512 devices in a mesh: req: 8 (over z), blk: 64 (over x, y, core).
Axes of the slice: x: 4, y: 8, z: 8, core: 2. Of those that a mesh axis runs over, the one named last changes fastest.
Arguments:
- tokens: bfloat16 [8, 512, 2048], P('req'), may hold values from -6 to 6
- cache_entries: bfloat16 [8, 64, 2048, 2, 128], P('req', 'blk'), may hold values from -1400 to 1400
- cache_tenants: int32 [8, 8192], P('req'), may hold values from 0 to 7
- cached_length: int32 [8], P('req'), may hold values from 2048 to 8192, as said below
- tenant_bounds: int32 [8, 2], P('req'), may hold values from 0 to 8, as said below
- qkv_weight: bfloat16 [2048, 3, 2048], P('req', None, 'blk'), may hold values from -0.125 to 0.125
- qkv_bias: float32 [3, 2048], P(None, 'blk'), may hold values from -3 to 3
- out_weight: bfloat16 [2048, 2048], P('req', 'blk'), may hold values from -0.125 to 0.125
- in_weight: bfloat16 [2048, 8192], P('req', 'blk'), may hold values from -0.125 to 0.125
- in_bias: float32 [8192], replicated, may hold values from -3 to 3
- down_weight: bfloat16 [2048, 8192], P('req', 'blk'), may hold values from -0.0625 to 0.0625
- out_biases: float32 [2, 2048], replicated, may hold values from -3 to 3
- norm_gains: float32 [2, 2048], replicated, may hold values from 0.5 to 1.5
- norm_biases: float32 [2, 2048], replicated, may hold values from -1.2 to 1.2
Outputs:
- layer_output: bfloat16 [8, 512, 2048], P('req', 'blk')
- appended: bfloat16 [8, 512, 2, 2048], P('req', None, None, 'blk')
The draws below stay inside these ranges and needn't reach their ends.
Inputs may be any that keep to these rules, and one draw needn't show every extreme that they name: `cached_length`: at least one request has exactly 8192 cached positions. `tenant_bounds`: the lower bound is below the upper one; some request's upper bound is 8 and some request's lower bound is 0.
All inputs are finite; a program needn't handle non-finite values.
Results may differ from the reference program's by a relative error of at most 0.015.
The reference program's roundings to bfloat16 on the way (of `qkv`, `keys`, `weights`, `context`, `projected`, `normed` and `inner`) count: a program that leaves them out, or rounds other values in their place, can miss the bound.
Values may be sent and summed in bfloat16 or wider, within the bound.
No kernel may reach another device: no remote copies, remote signals or barrier semaphores. Data moves between devices by JAX's collectives and lax.ppermute only.
A program may use at most 64 MiB of HBM per device.

```python
import math
import jax
import jax.numpy as jnp
from jax import lax

D = 2048
HEADS = 16
HEAD_DIM = 128
FF = 8192
TENANTS = 8
NEW = 512
CACHE_DEV = 2048
REQS = 8
GROUPS = 4
CACHE = 8192


def draw_cached_length(key, part):
    first_key, second_key = jax.random.split(key)
    lengths = jax.random.randint(first_key, (REQS,), CACHE // 4, CACHE + 1)
    chosen = jax.random.randint(second_key, (), 0, REQS)
    return jnp.where(jnp.arange(REQS) == chosen, CACHE, lengths).astype(jnp.int32)


def draw_tenant_bounds(key, part):
    first_key, second_key, third_key = jax.random.split(jax.random.fold_in(key, 11), 3)
    lower = jax.random.randint(first_key, (REQS,), 0, TENANTS // 2)
    spread = jax.random.randint(second_key, (REQS,), 2, TENANTS // 2 + 1)
    chosen = jax.random.randint(third_key, (), 0, REQS)
    request_index = jnp.arange(REQS)
    other = (chosen + 1) % REQS
    upper = jnp.where(request_index == chosen, TENANTS, lower + spread)
    lower = jnp.where((request_index == other) & (request_index != chosen), 0, lower)
    lower = jnp.where((REQS == 1) & (request_index == chosen), 0, lower)
    return jnp.stack([lower, upper], axis=1).astype(jnp.int32)


def draw_cache_entries(key, part):
    entries = jax.random.truncated_normal(key, -6.0, 6.0, (REQS, HEADS * GROUPS, CACHE_DEV, 2, HEAD_DIM), jnp.float32)
    return entries.astype(jnp.bfloat16)


def place_ends(values, rng, smallest, high):
    dims = values.shape
    index_at = [jax.random.randint(jax.random.fold_in(rng, axis), (), 0, dims[axis]) for axis in range(len(dims))]
    values = values.at[tuple(index_at)].set(smallest)
    longest = dims.index(max(dims))
    index_at[longest] = (index_at[longest] + 1) % dims[longest]
    return values.at[tuple(index_at)].set(high)


def steps_of(stream_key, extent, pieces, smallest, top_value):
    gain = 1.0
    for axis_at, shards_of in pieces:
        draws = jax.random.uniform(jax.random.fold_in(jax.random.fold_in(stream_key, 6), axis_at), (shards_of,), jnp.float32, smallest / len(pieces), top_value / len(pieces))
        gain = gain * jnp.repeat(jnp.exp(draws), extent[axis_at] // shards_of).reshape((-1,) + (1,) * (len(extent) - 1 - axis_at))
    return gain


def gaussian(rng, shape, deviation, bound, cuts=(), held_as=jnp.bfloat16):
    drawn = deviation * jax.random.normal(rng, shape, jnp.float32)
    if cuts:
        drawn = drawn * steps_of(rng, shape, cuts, -0.22, 0.18)
    return jnp.clip(drawn, -bound, bound).astype(held_as)


def setup_inputs(seed: int = 0) -> dict:
    keys = jax.random.split(jax.random.key(seed), 15)
    tokens = gaussian(keys[0], (REQS, NEW, D), 1.0, 6.0, ((0, 8),))
    cache_entries = draw_cache_entries(jax.random.fold_in(keys[14], 71), 0)
    cache_tenants = place_ends(jax.random.randint(keys[2], (REQS, CACHE), 0, TENANTS), jax.random.fold_in(keys[2], 1), 0, TENANTS - 1).astype(jnp.int32)
    cached_length = draw_cached_length(jax.random.fold_in(keys[14], 71), 0)
    tenant_bounds = draw_tenant_bounds(jax.random.fold_in(keys[14], 71), 0)
    qkv_weight = gaussian(keys[5], (D, 3, D), D ** -0.5, 0.125, ((0, 8), (2, 64)))
    qkv_bias = gaussian(keys[6], (3, D), 0.5, 3.0, ((1, 64),), jnp.float32)
    out_weight = gaussian(keys[7], (D, D), D ** -0.5, 0.125, ((0, 8), (1, 64)))
    in_weight = gaussian(keys[8], (D, FF), D ** -0.5, 0.125, ((0, 8), (1, 64)))
    in_bias = gaussian(keys[9], (FF,), 0.5, 3.0, (), jnp.float32)
    down_weight = gaussian(keys[10], (D, FF), FF ** -0.5, 0.0625, ((0, 8), (1, 64)))
    out_biases = gaussian(keys[11], (2, D), 0.5, 3.0, (), jnp.float32)
    norm_gains = jnp.clip(1.0 + 0.1 * jax.random.normal(keys[12], (2, D), jnp.float32), 0.5, 1.5)
    norm_biases = gaussian(keys[13], (2, D), 0.2, 1.2, (), jnp.float32)
    return dict(tokens=tokens, cache_entries=cache_entries, cache_tenants=cache_tenants, cached_length=cached_length, tenant_bounds=tenant_bounds, qkv_weight=qkv_weight, qkv_bias=qkv_bias, out_weight=out_weight, in_weight=in_weight, in_bias=in_bias, down_weight=down_weight, out_biases=out_biases, norm_gains=norm_gains, norm_biases=norm_biases)


def layer_norm(values, gain_row, shift_row):
    centered = values - lax.optimization_barrier(jnp.mean(values, axis=-1, keepdims=True))
    variance = lax.optimization_barrier(jnp.mean(centered * centered, axis=-1, keepdims=True))
    return centered * lax.rsqrt(variance + 1e-06) * gain_row + shift_row

def one_head(queries, key_rows, value_rows, visible):
    scores = jnp.dot(queries, key_rows.T, preferred_element_type=jnp.float32) * (1.0 / math.sqrt(HEAD_DIM))
    scores = jnp.where(visible, scores, -1e+30)
    row_max = lax.optimization_barrier(jnp.max(scores, axis=1, keepdims=True))
    weights = jnp.where(visible, jnp.exp(scores - row_max), 0.0)
    row_total = lax.optimization_barrier(jnp.sum(weights, axis=1, keepdims=True))
    numerator = jnp.dot(weights.astype(jnp.bfloat16), value_rows, preferred_element_type=jnp.float32)
    return numerator / row_total

def one_request(inputs):
    qkv_rows, cache_rows, tenant_row, length, bounds = inputs
    cache_heads = cache_rows.reshape(HEADS, CACHE, 2, HEAD_DIM)
    new_queries = qkv_rows[:, 0].reshape(NEW, HEADS, HEAD_DIM).transpose(1, 0, 2)
    new_keys = qkv_rows[:, 1].reshape(NEW, HEADS, HEAD_DIM).transpose(1, 0, 2)
    new_values = qkv_rows[:, 2].reshape(NEW, HEADS, HEAD_DIM).transpose(1, 0, 2)
    head_keys = jnp.concatenate([cache_heads[:, :, 0], new_keys], axis=1)
    head_values = jnp.concatenate([cache_heads[:, :, 1], new_values], axis=1)
    position = jnp.arange(CACHE, dtype=jnp.int32)
    readable = (position < length) & (tenant_row >= bounds[0]) & (tenant_row < bounds[1])
    query_index = jnp.arange(NEW, dtype=jnp.int32)
    causal = query_index[None, :] <= query_index[:, None]
    visible = jnp.concatenate([jnp.broadcast_to(readable[None, :], (NEW, CACHE)), causal], axis=1)
    context = lax.map(lambda triple: one_head(triple[0], triple[1], triple[2], visible), (new_queries, head_keys, head_values))
    return context.transpose(1, 0, 2).reshape(NEW, D).astype(jnp.bfloat16)

def reference(tokens, cache_entries, cache_tenants, cached_length, tenant_bounds, qkv_weight, qkv_bias, out_weight, in_weight, in_bias, down_weight, out_biases, norm_gains, norm_biases):
    flat_tokens = tokens.reshape(REQS * NEW, D)
    qkv = jnp.dot(flat_tokens, qkv_weight.reshape(D, 3 * D), preferred_element_type=jnp.float32) + qkv_bias.reshape(3 * D)
    qkv = qkv.astype(jnp.bfloat16).reshape(REQS, NEW, 3, D)
    appended = qkv[:, :, 1:]
    context = lax.map(one_request, (qkv, cache_entries, cache_tenants, cached_length, tenant_bounds))
    context = context.reshape(REQS * NEW, D)
    projected = (jnp.dot(context, out_weight, preferred_element_type=jnp.float32) + out_biases[0]).astype(jnp.bfloat16)
    normed = layer_norm(flat_tokens.astype(jnp.float32) + projected.astype(jnp.float32), norm_gains[0], norm_biases[0]).astype(jnp.bfloat16)
    inner = jax.nn.gelu(jnp.dot(normed, in_weight, preferred_element_type=jnp.float32) + in_bias, approximate=True).astype(jnp.bfloat16)
    mixed = jnp.dot(inner, down_weight.T, preferred_element_type=jnp.float32) + out_biases[1]
    layer_output = layer_norm(normed.astype(jnp.float32) + mixed, norm_gains[1], norm_biases[1]).astype(jnp.bfloat16)
    return (layer_output.reshape(REQS, NEW, D), appended)
```

```python
import math

import jax
import jax.numpy as jnp
from jax import lax
from jax.sharding import Mesh
from jax.sharding import PartitionSpec as P

HEADS = 16
HEAD_DIM = 128


MASKED = -1e30
PLANE = ("bx", "by")
BLK = ("bx", "by", "bc")


def swap(axis, n):
    return [(i, i ^ 1) for i in range(n)]


def layer_norm(values, gain_row, shift_row):
    centered = values - jnp.mean(values, axis=-1, keepdims=True)
    variance = jnp.mean(centered * centered, axis=-1, keepdims=True)
    return centered * lax.rsqrt(variance + 1e-06) * gain_row + shift_row


def partial_block(queries, key_rows, value_rows, visible):
    scores = jnp.einsum("qd,kd->qk", queries, key_rows, preferred_element_type=jnp.float32) * (
        1.0 / math.sqrt(HEAD_DIM)
    )
    scores = jnp.where(visible, scores, MASKED)
    row_max = jnp.max(scores, axis=1)
    weights = jnp.where(visible, jnp.exp(scores - row_max[:, None]), 0.0)
    row_total = jnp.sum(weights, axis=1)
    numerator = jnp.dot(
        weights.astype(jnp.bfloat16), value_rows, preferred_element_type=jnp.float32
    )
    return (numerator, row_max, row_total)


def merge_blocks(earlier_part, later_part):
    joined = jnp.maximum(earlier_part[1], later_part[1])
    scale_earlier = jnp.exp(earlier_part[1] - joined)
    scale_later = jnp.exp(later_part[1] - joined)
    numerator = earlier_part[0] * scale_earlier[:, None] + later_part[0] * scale_later[:, None]
    return (numerator, joined, earlier_part[2] * scale_earlier + later_part[2] * scale_later)


def core_pair(own, other, core, axis):
    return jnp.where(
        core == 0,
        jnp.concatenate([own, other], axis=axis),
        jnp.concatenate([other, own], axis=axis),
    )


def local(
    tokens,
    cache_entries,
    cache_tenants,
    cached_length,
    tenant_bounds,
    qkv_weight,
    qkv_bias,
    out_weight,
    in_weight,
    in_bias,
    down_weight,
    out_biases,
    norm_gains,
    norm_biases,
):
    nx, ny, nc = lax.axis_size("bx"), lax.axis_size("by"), lax.axis_size("bc")
    core = lax.axis_index("bc")
    chip = lax.axis_index("bx") * ny + lax.axis_index("by")
    block_index = chip * nc + core
    group_size = nx * ny * nc
    groups = group_size // HEADS
    low_bits = groups.bit_length() - 1
    group_index = block_index % groups

    rows, _, column_width = qkv_weight.shape
    qkv_flat = qkv_weight.reshape(rows, 3 * column_width)
    hidden_width = in_weight.shape[1]
    packed = jnp.concatenate([qkv_flat, out_weight, in_weight, down_weight], axis=1)
    full = lax.all_gather(packed, "req", axis=0, tiled=True)
    edges = [0, 3 * column_width, 4 * column_width, 4 * column_width + hidden_width]
    full_qkv = full[:, : edges[1]].reshape(-1, 3, column_width)
    late = full[:, edges[1] :]
    sibling = lax.ppermute(late, "bc", swap("bc", nc))
    chip_out = core_pair(late[:, :column_width], sibling[:, :column_width], core, 1)
    chip_in = jnp.concatenate(
        [late[:, column_width : column_width + hidden_width], sibling[:, column_width : column_width + hidden_width]],
        axis=1,
    )
    chip_down = jnp.concatenate(
        [late[:, column_width + hidden_width :], sibling[:, column_width + hidden_width :]], axis=1
    )
    sibling_block = block_index ^ 1
    chip_in_bias = jnp.concatenate(
        [
            lax.dynamic_slice_in_dim(in_bias, block_index * hidden_width, hidden_width),
            lax.dynamic_slice_in_dim(in_bias, sibling_block * hidden_width, hidden_width),
        ]
    )

    query_total = tokens.shape[1]
    token_rows = tokens[0]
    qkv_columns = (
        jnp.einsum("td,dce->tce", token_rows, full_qkv, preferred_element_type=jnp.float32)
        + qkv_bias
    ).astype(jnp.bfloat16)
    appended = qkv_columns[None, :, 1:]

    def from_partner(value, bit_level):
        if bit_level == 0:
            return lax.ppermute(value, "bc", swap("bc", nc))
        return lax.ppermute(value, "by", [(i, i ^ (1 << (bit_level - 1))) for i in range(ny)])

    head_qkv = qkv_columns
    for bit_level in range(low_bits):
        partner = from_partner(head_qkv, bit_level)
        upper_bit = group_index >> bit_level & 1
        head_qkv = jnp.where(
            upper_bit == 1,
            jnp.concatenate([partner, head_qkv], axis=2),
            jnp.concatenate([head_qkv, partner], axis=2),
        )
    queries = head_qkv[:, 0]
    fresh_count = query_total // groups
    fresh_start = group_index * fresh_count
    fresh_keys = lax.dynamic_slice_in_dim(head_qkv[:, 1], fresh_start, fresh_count, 0)
    fresh_values = lax.dynamic_slice_in_dim(head_qkv[:, 2], fresh_start, fresh_count, 0)
    cache_count = cache_entries.shape[2]
    cache_keys = cache_entries[0, 0, :, 0]
    cache_values = cache_entries[0, 0, :, 1]
    cache_position = group_index * cache_count + jnp.arange(cache_count, dtype=jnp.int32)
    tenant_slice = lax.dynamic_slice_in_dim(
        cache_tenants[0], group_index * cache_count, cache_count, 0
    )
    readable = (
        (cache_position < cached_length[0])
        & (tenant_slice >= tenant_bounds[0, 0])
        & (tenant_slice < tenant_bounds[0, 1])
    )
    query_position = jnp.arange(query_total, dtype=jnp.int32)
    fresh_position = fresh_start + jnp.arange(fresh_count, dtype=jnp.int32)
    fresh_visible = fresh_position[None, :] <= query_position[:, None]
    cache_visible = jnp.broadcast_to(readable[None, :], (query_total, cache_count))
    partial_value = partial_block(
        queries,
        jnp.concatenate([cache_keys, fresh_keys], axis=0),
        jnp.concatenate([cache_values, fresh_values], axis=0),
        jnp.concatenate([cache_visible, fresh_visible], axis=1),
    )
    numerator, row_max, row_total = partial_value
    for bit_level in reversed(range(low_bits)):
        halves = numerator.reshape(query_total, 2, -1)
        upper_bit = group_index >> bit_level & 1
        kept_half = jnp.where(upper_bit == 1, halves[:, 1], halves[:, 0])
        sent_half = jnp.where(upper_bit == 1, halves[:, 0], halves[:, 1])
        other_sum, other_max, other_total = from_partner((sent_half, row_max, row_total), bit_level)
        numerator, row_max, row_total = merge_blocks(
            (kept_half, row_max, row_total), (other_sum, other_max, other_total)
        )
    context_columns = (numerator / row_total[:, None]).astype(jnp.bfloat16)

    block_rows = query_total // (group_size)
    chips = nx * ny
    by_core = context_columns.reshape(chips, nc, block_rows, column_width)
    mine = lax.dynamic_index_in_dim(by_core, core, axis=1, keepdims=False)
    theirs = lax.dynamic_index_in_dim(by_core, 1 - core, axis=1, keepdims=False)
    got = lax.ppermute(theirs, "bc", swap("bc", nc))
    chip_context = core_pair(mine, got, core, 2).reshape(chips * block_rows, nc * column_width)
    core_context = lax.all_gather(chip_context, PLANE, axis=1, tiled=True)
    chip_width = nc * column_width
    column_bias = lax.dynamic_slice_in_dim(out_biases[0], chip * chip_width, chip_width)
    projected_part = (
        jnp.dot(core_context, chip_out, preferred_element_type=jnp.float32) + column_bias
    ).astype(jnp.bfloat16)
    projected = lax.all_gather(projected_part, PLANE, axis=1, tiled=True)
    core_tokens = lax.dynamic_index_in_dim(
        token_rows.reshape(chips, nc, block_rows, -1), core, axis=1, keepdims=False
    ).reshape(chips * block_rows, -1)
    normed = layer_norm(
        core_tokens.astype(jnp.float32) + projected.astype(jnp.float32),
        norm_gains[0],
        norm_biases[0],
    ).astype(jnp.bfloat16)
    inner = jax.nn.gelu(
        jnp.dot(normed, chip_in, preferred_element_type=jnp.float32) + chip_in_bias, approximate=True
    ).astype(jnp.bfloat16)
    mixed_rows = lax.psum_scatter(
        jnp.einsum("rf,df->rd", inner, chip_down, preferred_element_type=jnp.float32),
        PLANE,
        scatter_dimension=0,
        tiled=True,
    )
    own_normed = lax.dynamic_slice_in_dim(normed, chip * block_rows, block_rows, 0)
    layer_output = layer_norm(
        own_normed.astype(jnp.float32) + mixed_rows + out_biases[1], norm_gains[1], norm_biases[1]
    ).astype(jnp.bfloat16)
    return (layer_output[None], appended)


def solution(mesh):
    req, blk = mesh.devices.shape
    fine = Mesh(mesh.devices.reshape(req, 4, blk // 8, 2), ("req",) + BLK)
    return jax.shard_map(
        local,
        mesh=fine,
        in_specs=(
            P("req", None, None),
            P("req", BLK, None, None, None),
            P("req", None),
            P("req"),
            P("req", None),
            P("req", None, BLK),
            P(None, BLK),
            P("req", BLK),
            P("req", BLK),
            P(),
            P("req", BLK),
            P(),
            P(),
            P(),
        ),
        out_specs=(P("req", BLK, None), P("req", None, None, BLK)),
        check_vma=False,
    )
```

```python
import math

import jax
import jax.numpy as jnp
from jax import lax
from jax.sharding import Mesh
from jax.sharding import PartitionSpec as P

HEADS = 16
HEAD_DIM = 128


MASKED = -1e30
PLANE = ("bx", "by")
BLK = ("bx", "by", "bc")


def swap(axis, n):
    return [(i, i ^ 1) for i in range(n)]


def layer_norm(values, gain_row, shift_row):
    centered = values - jnp.mean(values, axis=-1, keepdims=True)
    variance = jnp.mean(centered * centered, axis=-1, keepdims=True)
    return centered * lax.rsqrt(variance + 1e-06) * gain_row + shift_row


def partial_block(queries, key_rows, value_rows, visible):
    scores = jnp.einsum("qd,kd->qk", queries, key_rows, preferred_element_type=jnp.float32) * (
        1.0 / math.sqrt(HEAD_DIM)
    )
    scores = jnp.where(visible, scores, MASKED)
    row_max = jnp.max(scores, axis=1)
    weights = jnp.where(visible, jnp.exp(scores - row_max[:, None]), 0.0)
    row_total = jnp.sum(weights, axis=1)
    numerator = jnp.dot(
        weights.astype(jnp.bfloat16), value_rows, preferred_element_type=jnp.float32
    )
    return (numerator, row_max, row_total)


def merge_blocks(earlier_part, later_part):
    joined = jnp.maximum(earlier_part[1], later_part[1])
    scale_earlier = jnp.exp(earlier_part[1] - joined)
    scale_later = jnp.exp(later_part[1] - joined)
    numerator = earlier_part[0] * scale_earlier[:, None] + later_part[0] * scale_later[:, None]
    return (numerator, joined, earlier_part[2] * scale_earlier + later_part[2] * scale_later)


def core_pair(own, other, core, axis):
    return jnp.where(
        core == 0,
        jnp.concatenate([own, other], axis=axis),
        jnp.concatenate([other, own], axis=axis),
    )


def local(
    tokens,
    cache_entries,
    cache_tenants,
    cached_length,
    tenant_bounds,
    qkv_weight,
    qkv_bias,
    out_weight,
    in_weight,
    in_bias,
    down_weight,
    out_biases,
    norm_gains,
    norm_biases,
):
    nx, ny, nc = lax.axis_size("bx"), lax.axis_size("by"), lax.axis_size("bc")
    core = lax.axis_index("bc")
    chip = lax.axis_index("bx") * ny + lax.axis_index("by")
    block_index = chip * nc + core
    group_size = nx * ny * nc
    groups = group_size // HEADS
    low_bits = groups.bit_length() - 1
    group_index = block_index % groups

    rows, _, column_width = qkv_weight.shape
    qkv_flat = qkv_weight.reshape(rows, 3 * column_width)
    hidden_width = in_weight.shape[1]
    full_qkv = lax.all_gather(qkv_flat, "req", axis=0, tiled=True).reshape(-1, 3, column_width)
    packed = jnp.concatenate([out_weight, in_weight, down_weight], axis=1)
    late = lax.all_gather(packed, "req", axis=0, tiled=True)
    sibling = lax.ppermute(late, "bc", swap("bc", nc))
    chip_out = core_pair(late[:, :column_width], sibling[:, :column_width], core, 1)
    chip_in = jnp.concatenate(
        [late[:, column_width : column_width + hidden_width], sibling[:, column_width : column_width + hidden_width]],
        axis=1,
    )
    chip_down = jnp.concatenate(
        [late[:, column_width + hidden_width :], sibling[:, column_width + hidden_width :]], axis=1
    )
    sibling_block = block_index ^ 1
    chip_in_bias = jnp.concatenate(
        [
            lax.dynamic_slice_in_dim(in_bias, block_index * hidden_width, hidden_width),
            lax.dynamic_slice_in_dim(in_bias, sibling_block * hidden_width, hidden_width),
        ]
    )

    query_total = tokens.shape[1]
    token_rows = tokens[0]
    qkv_columns = (
        jnp.einsum("td,dce->tce", token_rows, full_qkv, preferred_element_type=jnp.float32)
        + qkv_bias
    ).astype(jnp.bfloat16)
    appended = qkv_columns[None, :, 1:]

    def from_partner(value, bit_level):
        if bit_level == 0:
            return lax.ppermute(value, "bc", swap("bc", nc))
        return lax.ppermute(value, "by", [(i, i ^ (1 << (bit_level - 1))) for i in range(ny)])

    head_qkv = qkv_columns
    for bit_level in range(low_bits):
        partner = from_partner(head_qkv, bit_level)
        upper_bit = group_index >> bit_level & 1
        head_qkv = jnp.where(
            upper_bit == 1,
            jnp.concatenate([partner, head_qkv], axis=2),
            jnp.concatenate([head_qkv, partner], axis=2),
        )
    queries = head_qkv[:, 0]
    fresh_count = query_total // groups
    fresh_start = group_index * fresh_count
    fresh_keys = lax.dynamic_slice_in_dim(head_qkv[:, 1], fresh_start, fresh_count, 0)
    fresh_values = lax.dynamic_slice_in_dim(head_qkv[:, 2], fresh_start, fresh_count, 0)
    cache_count = cache_entries.shape[2]
    cache_keys = cache_entries[0, 0, :, 0]
    cache_values = cache_entries[0, 0, :, 1]
    cache_position = group_index * cache_count + jnp.arange(cache_count, dtype=jnp.int32)
    tenant_slice = lax.dynamic_slice_in_dim(
        cache_tenants[0], group_index * cache_count, cache_count, 0
    )
    readable = (
        (cache_position < cached_length[0])
        & (tenant_slice >= tenant_bounds[0, 0])
        & (tenant_slice < tenant_bounds[0, 1])
    )
    query_position = jnp.arange(query_total, dtype=jnp.int32)
    fresh_position = fresh_start + jnp.arange(fresh_count, dtype=jnp.int32)
    fresh_visible = fresh_position[None, :] <= query_position[:, None]
    cache_visible = jnp.broadcast_to(readable[None, :], (query_total, cache_count))
    partial_value = partial_block(
        queries,
        jnp.concatenate([cache_keys, fresh_keys], axis=0),
        jnp.concatenate([cache_values, fresh_values], axis=0),
        jnp.concatenate([cache_visible, fresh_visible], axis=1),
    )
    numerator, row_max, row_total = partial_value
    for bit_level in reversed(range(low_bits)):
        halves = numerator.reshape(query_total, 2, -1)
        upper_bit = group_index >> bit_level & 1
        kept_half = jnp.where(upper_bit == 1, halves[:, 1], halves[:, 0])
        sent_half = jnp.where(upper_bit == 1, halves[:, 0], halves[:, 1])
        sent = jnp.concatenate([sent_half, row_max[:, None], row_total[:, None]], axis=1)
        got_back = from_partner(sent, bit_level)
        other_sum, other_max, other_total = got_back[:, :-2], got_back[:, -2], got_back[:, -1]
        numerator, row_max, row_total = merge_blocks(
            (kept_half, row_max, row_total), (other_sum, other_max, other_total)
        )
    context_columns = (numerator / row_total[:, None]).astype(jnp.bfloat16)

    block_rows = query_total // (group_size)
    chips = nx * ny
    by_core = context_columns.reshape(chips, nc, block_rows, column_width)
    halves = by_core.transpose(1, 0, 2, 3).reshape(nc, chips * block_rows, column_width)
    outgoing = jnp.broadcast_to(halves[None], (chips, nc, chips * block_rows, column_width))
    incoming = lax.all_to_all(
        outgoing.reshape(group_size, chips * block_rows, column_width), BLK, 0, 0, tiled=True
    )
    core_context = incoming.transpose(1, 0, 2).reshape(chips * block_rows, group_size * column_width)
    chip_width = nc * column_width
    column_bias = lax.dynamic_slice_in_dim(out_biases[0], chip * chip_width, chip_width)
    projected_part = (
        jnp.dot(core_context, chip_out, preferred_element_type=jnp.float32) + column_bias
    ).astype(jnp.bfloat16)
    spread = jnp.broadcast_to(projected_part[None], (chips,) + projected_part.shape)
    projected = (
        lax.all_to_all(spread, PLANE, 0, 0, tiled=True)
        .transpose(1, 0, 2)
        .reshape(projected_part.shape[0], chips * chip_width)
    )
    core_tokens = lax.dynamic_index_in_dim(
        token_rows.reshape(chips, nc, block_rows, -1), core, axis=1, keepdims=False
    ).reshape(chips * block_rows, -1)
    normed = layer_norm(
        core_tokens.astype(jnp.float32) + projected.astype(jnp.float32),
        norm_gains[0],
        norm_biases[0],
    ).astype(jnp.bfloat16)
    inner = jax.nn.gelu(
        jnp.dot(normed, chip_in, preferred_element_type=jnp.float32) + chip_in_bias, approximate=True
    ).astype(jnp.bfloat16)
    mixed_parts = jnp.einsum("rf,df->rd", inner, chip_down, preferred_element_type=jnp.float32)
    mixed_rows = lax.all_to_all(
        mixed_parts.reshape(chips, block_rows, -1), PLANE, 0, 0, tiled=True
    ).sum(axis=0)
    own_normed = lax.dynamic_slice_in_dim(normed, chip * block_rows, block_rows, 0)
    layer_output = layer_norm(
        own_normed.astype(jnp.float32) + mixed_rows + out_biases[1], norm_gains[1], norm_biases[1]
    ).astype(jnp.bfloat16)
    return (layer_output[None], appended)


def solution(mesh):
    req, blk = mesh.devices.shape
    fine = Mesh(mesh.devices.reshape(req, 4, blk // 8, 2), ("req",) + BLK)
    return jax.shard_map(
        local,
        mesh=fine,
        in_specs=(
            P("req", None, None),
            P("req", BLK, None, None, None),
            P("req", None),
            P("req"),
            P("req", None),
            P("req", None, BLK),
            P(None, BLK),
            P("req", BLK),
            P("req", BLK),
            P(),
            P("req", BLK),
            P(),
            P(),
            P(),
        ),
        out_specs=(P("req", BLK, None), P("req", None, None, BLK)),
        check_vma=False,
    )
```

```python
import math

import jax
import jax.numpy as jnp
from jax import lax
from jax.sharding import Mesh
from jax.sharding import PartitionSpec as P

HEADS = 16
HEAD_DIM = 128


MASKED = -1e30
PLANE = ("bx", "by")
BLK = ("bx", "by", "bc")


def swap(axis, n):
    return [(i, i ^ 1) for i in range(n)]


def layer_norm(values, gain_row, shift_row):
    centered = values - jnp.mean(values, axis=-1, keepdims=True)
    variance = jnp.mean(centered * centered, axis=-1, keepdims=True)
    return centered * lax.rsqrt(variance + 1e-06) * gain_row + shift_row


def partial_block(queries, key_rows, value_rows, visible):
    scores = jnp.einsum("qd,kd->qk", queries, key_rows, preferred_element_type=jnp.float32) * (
        1.0 / math.sqrt(HEAD_DIM)
    )
    scores = jnp.where(visible, scores, MASKED)
    row_max = jnp.max(scores, axis=1)
    weights = jnp.where(visible, jnp.exp(scores - row_max[:, None]), 0.0)
    row_total = jnp.sum(weights, axis=1)
    numerator = jnp.einsum(
        "qk,kd->dq", weights.astype(jnp.bfloat16), value_rows, preferred_element_type=jnp.float32
    )
    return (numerator, row_max, row_total)


def merge_blocks(earlier_part, later_part):
    joined = jnp.maximum(earlier_part[1], later_part[1])
    scale_earlier = jnp.exp(earlier_part[1] - joined)
    scale_later = jnp.exp(later_part[1] - joined)
    numerator = earlier_part[0] * scale_earlier[:, None] + later_part[0] * scale_later[:, None]
    return (numerator, joined, earlier_part[2] * scale_earlier + later_part[2] * scale_later)


def gather_rows(block):
    reqs = lax.axis_size("req")
    spread = jnp.broadcast_to(block[None], (reqs,) + block.shape)
    return lax.all_to_all(spread, "req", 0, 0, tiled=True).reshape(reqs * block.shape[0], -1)


def core_pair(own, other, core, axis):
    return jnp.where(
        core == 0,
        jnp.concatenate([own, other], axis=axis),
        jnp.concatenate([other, own], axis=axis),
    )


def local(
    tokens,
    cache_entries,
    cache_tenants,
    cached_length,
    tenant_bounds,
    qkv_weight,
    qkv_bias,
    out_weight,
    in_weight,
    in_bias,
    down_weight,
    out_biases,
    norm_gains,
    norm_biases,
):
    nx, ny, nc = lax.axis_size("bx"), lax.axis_size("by"), lax.axis_size("bc")
    core = lax.axis_index("bc")
    chip = lax.axis_index("bx") * ny + lax.axis_index("by")
    block_index = chip * nc + core
    group_size = nx * ny * nc
    groups = group_size // HEADS
    low_bits = groups.bit_length() - 1
    group_index = block_index % groups

    rows, _, column_width = qkv_weight.shape
    qkv_flat = qkv_weight.reshape(rows, 3 * column_width)
    hidden_width = in_weight.shape[1]
    packed = jnp.concatenate([out_weight, in_weight, down_weight], axis=1)
    full_qkv = gather_rows(qkv_flat).reshape(-1, 3, column_width)
    late = gather_rows(packed)
    sibling = lax.ppermute(late, "bc", swap("bc", nc))
    chip_out = core_pair(late[:, :column_width], sibling[:, :column_width], core, 1)
    chip_in = jnp.concatenate(
        [late[:, column_width : column_width + hidden_width], sibling[:, column_width : column_width + hidden_width]],
        axis=1,
    )
    chip_down = jnp.concatenate(
        [late[:, column_width + hidden_width :], sibling[:, column_width + hidden_width :]], axis=1
    )
    sibling_block = block_index ^ 1
    chip_in_bias = jnp.concatenate(
        [
            lax.dynamic_slice_in_dim(in_bias, block_index * hidden_width, hidden_width),
            lax.dynamic_slice_in_dim(in_bias, sibling_block * hidden_width, hidden_width),
        ]
    )

    query_total = tokens.shape[1]
    token_rows = tokens[0]
    qkv_columns = (
        jnp.einsum("td,dce->cet", token_rows, full_qkv, preferred_element_type=jnp.float32)
        + qkv_bias[:, :, None]
    ).astype(jnp.bfloat16)
    appended = qkv_columns[1:].transpose(2, 0, 1)[None]

    def from_partner(value, bit_level):
        if bit_level == 0:
            return lax.ppermute(value, "bc", swap("bc", nc))
        return lax.ppermute(value, "by", [(i, i ^ (1 << (bit_level - 1))) for i in range(ny)])

    head_qkv = qkv_columns
    for bit_level in range(low_bits):
        partner = from_partner(head_qkv, bit_level)
        upper_bit = group_index >> bit_level & 1
        head_qkv = jnp.where(
            upper_bit == 1,
            jnp.concatenate([partner, head_qkv], axis=1),
            jnp.concatenate([head_qkv, partner], axis=1),
        )
    queries = head_qkv[0].T
    fresh_count = query_total // groups
    fresh_start = group_index * fresh_count
    fresh_keys = lax.dynamic_slice_in_dim(head_qkv[1], fresh_start, fresh_count, 1).T
    fresh_values = lax.dynamic_slice_in_dim(head_qkv[2], fresh_start, fresh_count, 1).T
    cache_count = cache_entries.shape[2]
    cache_keys = cache_entries[0, 0, :, 0]
    cache_values = cache_entries[0, 0, :, 1]
    cache_position = group_index * cache_count + jnp.arange(cache_count, dtype=jnp.int32)
    tenant_slice = lax.dynamic_slice_in_dim(
        cache_tenants[0], group_index * cache_count, cache_count, 0
    )
    readable = (
        (cache_position < cached_length[0])
        & (tenant_slice >= tenant_bounds[0, 0])
        & (tenant_slice < tenant_bounds[0, 1])
    )
    query_position = jnp.arange(query_total, dtype=jnp.int32)
    fresh_position = fresh_start + jnp.arange(fresh_count, dtype=jnp.int32)
    fresh_visible = fresh_position[None, :] <= query_position[:, None]
    cache_visible = jnp.broadcast_to(readable[None, :], (query_total, cache_count))
    numerator, row_max, row_total = partial_block(
        queries,
        jnp.concatenate([cache_keys, fresh_keys], axis=0),
        jnp.concatenate([cache_values, fresh_values], axis=0),
        jnp.concatenate([cache_visible, fresh_visible], axis=1),
    )
    for bit_level in reversed(range(low_bits)):
        halves = numerator.reshape(2, -1, query_total)
        upper_bit = group_index >> bit_level & 1
        kept_half = jnp.where(upper_bit == 1, halves[1], halves[0])
        sent_half = jnp.where(upper_bit == 1, halves[0], halves[1])
        sent = jnp.concatenate([sent_half, row_max[None], row_total[None]], axis=0)
        got_back = from_partner(sent, bit_level)
        other_sum, other_max, other_total = got_back[:-2], got_back[-2], got_back[-1]
        joined = jnp.maximum(row_max, other_max)
        scale_kept = jnp.exp(row_max - joined)
        scale_other = jnp.exp(other_max - joined)
        numerator = kept_half * scale_kept[None] + other_sum * scale_other[None]
        row_max, row_total = joined, row_total * scale_kept + other_total * scale_other
    context_columns = (numerator / row_total[None]).astype(jnp.bfloat16)

    block_rows = query_total // (group_size)
    chips = nx * ny
    core_rows = chips * block_rows
    halves = (
        context_columns.reshape(column_width, chips, nc, block_rows)
        .transpose(2, 0, 1, 3)
        .reshape(nc, column_width, core_rows)
    )
    outgoing = jnp.broadcast_to(halves[None], (chips, nc, column_width, core_rows))
    core_context = lax.all_to_all(
        outgoing.reshape(group_size, column_width, core_rows), BLK, 0, 0, tiled=True
    ).reshape(group_size * column_width, core_rows)
    chip_width = nc * column_width
    column_bias = lax.dynamic_slice_in_dim(out_biases[0], chip * chip_width, chip_width)
    projected_part = (
        jnp.einsum("ct,cd->dt", core_context, chip_out, preferred_element_type=jnp.float32)
        + column_bias[:, None]
    ).astype(jnp.bfloat16)
    spread = jnp.broadcast_to(projected_part[None], (chips,) + projected_part.shape)
    projected = lax.all_to_all(spread, PLANE, 0, 0, tiled=True).reshape(chips * chip_width, core_rows).T
    core_tokens = lax.dynamic_index_in_dim(
        token_rows.reshape(chips, nc, block_rows, -1), core, axis=1, keepdims=False
    ).reshape(chips * block_rows, -1)
    normed = layer_norm(
        core_tokens.astype(jnp.float32) + projected.astype(jnp.float32),
        norm_gains[0],
        norm_biases[0],
    ).astype(jnp.bfloat16)
    inner = jax.nn.gelu(
        jnp.dot(normed, chip_in, preferred_element_type=jnp.float32) + chip_in_bias, approximate=True
    ).astype(jnp.bfloat16)
    mixed_parts = jnp.einsum("rf,df->rd", inner, chip_down, preferred_element_type=jnp.float32)
    mixed_rows = lax.all_to_all(
        mixed_parts.reshape(chips, block_rows, -1), PLANE, 0, 0, tiled=True
    ).sum(axis=0)
    own_normed = lax.dynamic_slice_in_dim(normed, chip * block_rows, block_rows, 0)
    layer_output = layer_norm(
        own_normed.astype(jnp.float32) + mixed_rows + out_biases[1], norm_gains[1], norm_biases[1]
    ).astype(jnp.bfloat16)
    return (layer_output[None], appended)


def solution(mesh):
    req, blk = mesh.devices.shape
    fine = Mesh(mesh.devices.reshape(req, 4, blk // 8, 2), ("req",) + BLK)
    return jax.shard_map(
        local,
        mesh=fine,
        in_specs=(
            P("req", None, None),
            P("req", BLK, None, None, None),
            P("req", None),
            P("req"),
            P("req", None),
            P("req", None, BLK),
            P(None, BLK),
            P("req", BLK),
            P("req", BLK),
            P(),
            P("req", BLK),
            P(),
            P(),
            P(),
        ),
        out_specs=(P("req", BLK, None), P("req", None, None, BLK)),
        check_vma=False,
    )
```

```python
import math

import jax
import jax.numpy as jnp
from jax import lax
from jax.sharding import Mesh
from jax.sharding import PartitionSpec as P

HEADS = 16
HEAD_DIM = 128


MASKED = -1e30
PLANE = ("bx", "by")
BLK = ("bx", "by", "bc")


def swap(axis, n):
    return [(i, i ^ 1) for i in range(n)]


def layer_norm(values, gain_row, shift_row):
    centered = values - jnp.mean(values, axis=-1, keepdims=True)
    variance = jnp.mean(centered * centered, axis=-1, keepdims=True)
    return centered * lax.rsqrt(variance + 1e-06) * gain_row + shift_row


def partial_block(queries, key_rows, value_rows, visible):
    scores = jnp.einsum("qd,kd->qk", queries, key_rows, preferred_element_type=jnp.float32) * (
        1.0 / math.sqrt(HEAD_DIM)
    )
    scores = jnp.where(visible, scores, MASKED)
    row_max = jnp.max(scores, axis=1)
    weights = jnp.where(visible, jnp.exp(scores - row_max[:, None]), 0.0)
    row_total = jnp.sum(weights, axis=1)
    numerator = jnp.einsum(
        "qk,kd->dq", weights.astype(jnp.bfloat16), value_rows, preferred_element_type=jnp.float32
    )
    return (numerator, row_max, row_total)


def gather_rows(block):
    reqs = lax.axis_size("req")
    spread = jnp.broadcast_to(block[None], (reqs,) + block.shape)
    return lax.all_to_all(spread, "req", 0, 0, tiled=True).reshape(reqs * block.shape[0], -1)


def core_pair(own, other, core, axis):
    return jnp.where(
        core == 0,
        jnp.concatenate([own, other], axis=axis),
        jnp.concatenate([other, own], axis=axis),
    )


def local(
    tokens,
    cache_entries,
    cache_tenants,
    cached_length,
    tenant_bounds,
    qkv_weight,
    qkv_bias,
    out_weight,
    in_weight,
    in_bias,
    down_weight,
    out_biases,
    norm_gains,
    norm_biases,
):
    nx, ny, nc = lax.axis_size("bx"), lax.axis_size("by"), lax.axis_size("bc")
    core = lax.axis_index("bc")
    chip = lax.axis_index("bx") * ny + lax.axis_index("by")
    block_index = chip * nc + core
    group_size = nx * ny * nc
    groups = group_size // HEADS
    group_index = block_index % groups

    rows, _, column_width = qkv_weight.shape
    qkv_flat = qkv_weight.reshape(rows, 3 * column_width)
    hidden_width = in_weight.shape[1]
    packed = jnp.concatenate([out_weight, in_weight, down_weight], axis=1)
    full_qkv = gather_rows(qkv_flat).reshape(-1, 3, column_width)
    late = gather_rows(packed)
    sibling = lax.ppermute(late, "bc", swap("bc", nc))
    chip_out = core_pair(late[:, :column_width], sibling[:, :column_width], core, 1)
    chip_in = jnp.concatenate(
        [late[:, column_width : column_width + hidden_width], sibling[:, column_width : column_width + hidden_width]],
        axis=1,
    )
    chip_down = jnp.concatenate(
        [late[:, column_width + hidden_width :], sibling[:, column_width + hidden_width :]], axis=1
    )
    sibling_block = block_index ^ 1
    chip_in_bias = jnp.concatenate(
        [
            lax.dynamic_slice_in_dim(in_bias, block_index * hidden_width, hidden_width),
            lax.dynamic_slice_in_dim(in_bias, sibling_block * hidden_width, hidden_width),
        ]
    )

    query_total = tokens.shape[1]
    token_rows = tokens[0]
    qkv_columns = (
        jnp.einsum("td,dce->cet", token_rows, full_qkv, preferred_element_type=jnp.float32)
        + qkv_bias[:, :, None]
    ).astype(jnp.bfloat16)
    appended = qkv_columns[1:].transpose(2, 0, 1)[None]

    quarter = query_total // groups
    members = ny * nc

    def from_member(value, k):
        return lax.ppermute(value, ("by", "bc"), [(i, i ^ k) for i in range(members)])

    own_kv = qkv_columns[1:]

    def outgoing_for(target):
        part = lax.dynamic_slice_in_dim(own_kv, target * quarter, quarter, 2)
        return jnp.concatenate(
            [qkv_columns[0], part.transpose(1, 0, 2).reshape(column_width, 2 * quarter)], axis=1
        )

    sources = [outgoing_for(group_index)]
    for k in range(1, groups):
        sources.append(from_member(outgoing_for(group_index ^ k), k))
    ordered = jnp.take(jnp.stack(sources), group_index ^ jnp.arange(groups), axis=0)
    head_q = ordered[:, :, :query_total].reshape(groups * column_width, query_total)
    head_kv = (
        ordered[:, :, query_total:]
        .reshape(groups, column_width, 2, quarter)
        .transpose(2, 0, 1, 3)
        .reshape(2, groups * column_width, quarter)
    )
    queries = head_q.T
    fresh_count = quarter
    fresh_keys = head_kv[0].T
    fresh_values = head_kv[1].T
    fresh_start = group_index * fresh_count
    cache_count = cache_entries.shape[2]
    cache_keys = cache_entries[0, 0, :, 0]
    cache_values = cache_entries[0, 0, :, 1]
    cache_position = group_index * cache_count + jnp.arange(cache_count, dtype=jnp.int32)
    tenant_slice = lax.dynamic_slice_in_dim(
        cache_tenants[0], group_index * cache_count, cache_count, 0
    )
    readable = (
        (cache_position < cached_length[0])
        & (tenant_slice >= tenant_bounds[0, 0])
        & (tenant_slice < tenant_bounds[0, 1])
    )
    query_position = jnp.arange(query_total, dtype=jnp.int32)
    fresh_position = fresh_start + jnp.arange(fresh_count, dtype=jnp.int32)
    fresh_visible = fresh_position[None, :] <= query_position[:, None]
    cache_visible = jnp.broadcast_to(readable[None, :], (query_total, cache_count))
    numerator, row_max, row_total = partial_block(
        queries,
        jnp.concatenate([cache_keys, fresh_keys], axis=0),
        jnp.concatenate([cache_values, fresh_values], axis=0),
        jnp.concatenate([cache_visible, fresh_visible], axis=1),
    )
    def stats_for(target):
        part = lax.dynamic_slice_in_dim(numerator, target * column_width, column_width, 0)
        return jnp.concatenate([part, row_max[None], row_total[None]], axis=0)

    pieces = [stats_for(group_index)]
    for k in range(1, groups):
        pieces.append(from_member(stats_for(group_index ^ k), k))
    maxima = jnp.stack([piece[-2] for piece in pieces])
    joined = jnp.max(maxima, axis=0)
    scales = jnp.exp(maxima - joined[None])
    numerator = pieces[0][:-2] * scales[0][None]
    row_total = pieces[0][-1] * scales[0]
    for k in range(1, groups):
        numerator = numerator + pieces[k][:-2] * scales[k][None]
        row_total = row_total + pieces[k][-1] * scales[k]
    context_columns = (numerator / row_total[None]).astype(jnp.bfloat16)

    block_rows = query_total // (group_size)
    chips = nx * ny
    core_rows = chips * block_rows
    halves = (
        context_columns.reshape(column_width, chips, nc, block_rows)
        .transpose(2, 0, 1, 3)
        .reshape(nc, column_width, core_rows)
    )
    outgoing = jnp.broadcast_to(halves[None], (chips, nc, column_width, core_rows))
    core_context = lax.all_to_all(
        outgoing.reshape(group_size, column_width, core_rows), BLK, 0, 0, tiled=True
    ).reshape(group_size * column_width, core_rows)
    chip_width = nc * column_width
    column_bias = lax.dynamic_slice_in_dim(out_biases[0], chip * chip_width, chip_width)
    projected_part = (
        jnp.einsum("ct,cd->dt", core_context, chip_out, preferred_element_type=jnp.float32)
        + column_bias[:, None]
    ).astype(jnp.bfloat16)
    spread = jnp.broadcast_to(projected_part[None], (chips,) + projected_part.shape)
    projected = lax.all_to_all(spread, PLANE, 0, 0, tiled=True).reshape(chips * chip_width, core_rows).T
    core_tokens = lax.dynamic_index_in_dim(
        token_rows.reshape(chips, nc, block_rows, -1), core, axis=1, keepdims=False
    ).reshape(chips * block_rows, -1)
    normed = layer_norm(
        core_tokens.astype(jnp.float32) + projected.astype(jnp.float32),
        norm_gains[0],
        norm_biases[0],
    ).astype(jnp.bfloat16)
    inner = jax.nn.gelu(
        jnp.dot(normed, chip_in, preferred_element_type=jnp.float32) + chip_in_bias, approximate=True
    ).astype(jnp.bfloat16)
    mixed_parts = jnp.einsum("rf,df->rd", inner, chip_down, preferred_element_type=jnp.float32)
    mixed_rows = lax.all_to_all(
        mixed_parts.reshape(chips, block_rows, -1), PLANE, 0, 0, tiled=True
    ).sum(axis=0)
    own_normed = lax.dynamic_slice_in_dim(normed, chip * block_rows, block_rows, 0)
    layer_output = layer_norm(
        own_normed.astype(jnp.float32) + mixed_rows + out_biases[1], norm_gains[1], norm_biases[1]
    ).astype(jnp.bfloat16)
    return (layer_output[None], appended)


def solution(mesh):
    req, blk = mesh.devices.shape
    fine = Mesh(mesh.devices.reshape(req, 4, blk // 8, 2), ("req",) + BLK)
    return jax.shard_map(
        local,
        mesh=fine,
        in_specs=(
            P("req", None, None),
            P("req", BLK, None, None, None),
            P("req", None),
            P("req"),
            P("req", None),
            P("req", None, BLK),
            P(None, BLK),
            P("req", BLK),
            P("req", BLK),
            P(),
            P("req", BLK),
            P(),
            P(),
            P(),
        ),
        out_specs=(P("req", BLK, None), P("req", None, None, BLK)),
        check_vma=False,
    )
```

```python
import math

import jax
import jax.numpy as jnp
from jax import lax
from jax.sharding import Mesh
from jax.sharding import PartitionSpec as P

HEADS = 16
HEAD_DIM = 128


MASKED = -1e30
PLANE = ("bx", "by")
BLK = ("bx", "by", "bc")


def swap(axis, n):
    return [(i, i ^ 1) for i in range(n)]


def layer_norm(values, gain_row, shift_row):
    centered = values - jnp.mean(values, axis=-1, keepdims=True)
    variance = jnp.mean(centered * centered, axis=-1, keepdims=True)
    return centered * lax.rsqrt(variance + 1e-06) * gain_row + shift_row


def partial_block(queries, key_rows, value_rows, visible):
    scores = jnp.einsum("qd,kd->qk", queries, key_rows, preferred_element_type=jnp.float32) * (
        1.0 / math.sqrt(HEAD_DIM)
    )
    scores = jnp.where(visible, scores, MASKED)
    row_max = jnp.max(scores, axis=1)
    weights = jnp.where(visible, jnp.exp(scores - row_max[:, None]), 0.0)
    row_total = jnp.sum(weights, axis=1)
    numerator = jnp.einsum(
        "qk,kd->dq", weights.astype(jnp.bfloat16), value_rows, preferred_element_type=jnp.float32
    )
    return (numerator, row_max, row_total)


def merge_blocks(earlier_part, later_part):
    joined = jnp.maximum(earlier_part[1], later_part[1])
    scale_earlier = jnp.exp(earlier_part[1] - joined)
    scale_later = jnp.exp(later_part[1] - joined)
    numerator = earlier_part[0] * scale_earlier[:, None] + later_part[0] * scale_later[:, None]
    return (numerator, joined, earlier_part[2] * scale_earlier + later_part[2] * scale_later)


def gather_rows(block):
    reqs = lax.axis_size("req")
    spread = jnp.broadcast_to(block[None], (reqs,) + block.shape)
    return lax.all_to_all(spread, "req", 0, 0, tiled=True).reshape(reqs * block.shape[0], -1)


def core_pair(own, other, core, axis):
    return jnp.where(
        core == 0,
        jnp.concatenate([own, other], axis=axis),
        jnp.concatenate([other, own], axis=axis),
    )


def local(
    tokens,
    cache_entries,
    cache_tenants,
    cached_length,
    tenant_bounds,
    qkv_weight,
    qkv_bias,
    out_weight,
    in_weight,
    in_bias,
    down_weight,
    out_biases,
    norm_gains,
    norm_biases,
):
    nx, ny, nc = lax.axis_size("bx"), lax.axis_size("by"), lax.axis_size("bc")
    core = lax.axis_index("bc")
    chip = lax.axis_index("bx") * ny + lax.axis_index("by")
    block_index = chip * nc + core
    group_size = nx * ny * nc
    groups = group_size // HEADS
    low_bits = groups.bit_length() - 1
    group_index = block_index % groups

    rows, _, column_width = qkv_weight.shape
    qkv_flat = qkv_weight.reshape(rows, 3 * column_width)
    hidden_width = in_weight.shape[1]
    packed = jnp.concatenate([out_weight, in_weight, down_weight], axis=1)
    full_qkv = gather_rows(qkv_flat).reshape(-1, 3, column_width)
    late = gather_rows(packed)
    front = late[:, : column_width + hidden_width]
    sibling = lax.ppermute(front, "bc", swap("bc", nc))
    chip_out = core_pair(front[:, :column_width], sibling[:, :column_width], core, 1)
    chip_in = core_pair(front[:, column_width:], sibling[:, column_width:], core, 1)
    chip_in_bias = lax.dynamic_slice_in_dim(in_bias, chip * nc * hidden_width, nc * hidden_width)
    d_model = late.shape[0]
    quarter_width = d_model // nx
    own_down = late[:, column_width + hidden_width :].reshape(nx, 1, quarter_width, hidden_width)
    group_down = lax.all_to_all(
        jnp.broadcast_to(own_down, (nx, nc, quarter_width, hidden_width)).reshape(
            nx * nc, quarter_width, hidden_width
        ),
        ("bx", "bc"),
        0,
        0,
        tiled=True,
    ).reshape(nx, nc, quarter_width, hidden_width)

    query_total = tokens.shape[1]
    token_rows = tokens[0]
    qkv_columns = (
        jnp.einsum("td,dce->cet", token_rows, full_qkv, preferred_element_type=jnp.float32)
        + qkv_bias[:, :, None]
    ).astype(jnp.bfloat16)
    appended = qkv_columns[1:].transpose(2, 0, 1)[None]

    def from_partner(value, bit_level):
        if bit_level == 0:
            return lax.ppermute(value, "bc", swap("bc", nc))
        return lax.ppermute(value, "by", [(i, i ^ (1 << (bit_level - 1))) for i in range(ny)])

    head_qkv = qkv_columns
    for bit_level in range(low_bits):
        partner = from_partner(head_qkv, bit_level)
        upper_bit = group_index >> bit_level & 1
        head_qkv = jnp.where(
            upper_bit == 1,
            jnp.concatenate([partner, head_qkv], axis=1),
            jnp.concatenate([head_qkv, partner], axis=1),
        )
    queries = head_qkv[0].T
    fresh_count = query_total // groups
    fresh_start = group_index * fresh_count
    fresh_keys = lax.dynamic_slice_in_dim(head_qkv[1], fresh_start, fresh_count, 1).T
    fresh_values = lax.dynamic_slice_in_dim(head_qkv[2], fresh_start, fresh_count, 1).T
    cache_count = cache_entries.shape[2]
    cache_keys = cache_entries[0, 0, :, 0]
    cache_values = cache_entries[0, 0, :, 1]
    cache_position = group_index * cache_count + jnp.arange(cache_count, dtype=jnp.int32)
    tenant_slice = lax.dynamic_slice_in_dim(
        cache_tenants[0], group_index * cache_count, cache_count, 0
    )
    readable = (
        (cache_position < cached_length[0])
        & (tenant_slice >= tenant_bounds[0, 0])
        & (tenant_slice < tenant_bounds[0, 1])
    )
    query_position = jnp.arange(query_total, dtype=jnp.int32)
    fresh_position = fresh_start + jnp.arange(fresh_count, dtype=jnp.int32)
    fresh_visible = fresh_position[None, :] <= query_position[:, None]
    cache_visible = jnp.broadcast_to(readable[None, :], (query_total, cache_count))
    numerator, row_max, row_total = partial_block(
        queries,
        jnp.concatenate([cache_keys, fresh_keys], axis=0),
        jnp.concatenate([cache_values, fresh_values], axis=0),
        jnp.concatenate([cache_visible, fresh_visible], axis=1),
    )
    for bit_level in reversed(range(low_bits)):
        halves = numerator.reshape(2, -1, query_total)
        upper_bit = group_index >> bit_level & 1
        kept_half = jnp.where(upper_bit == 1, halves[1], halves[0])
        sent_half = jnp.where(upper_bit == 1, halves[0], halves[1])
        sent = jnp.concatenate([sent_half, row_max[None], row_total[None]], axis=0)
        got_back = from_partner(sent, bit_level)
        other_sum, other_max, other_total = got_back[:-2], got_back[-2], got_back[-1]
        joined = jnp.maximum(row_max, other_max)
        scale_kept = jnp.exp(row_max - joined)
        scale_other = jnp.exp(other_max - joined)
        numerator = kept_half * scale_kept[None] + other_sum * scale_other[None]
        row_max, row_total = joined, row_total * scale_kept + other_total * scale_other
    context_columns = (numerator / row_total[None]).astype(jnp.bfloat16)

    block_rows = query_total // (group_size)
    chips = nx * ny
    core_rows = chips * block_rows
    halves = (
        context_columns.reshape(column_width, chips, nc, block_rows)
        .transpose(2, 0, 1, 3)
        .reshape(nc, column_width, core_rows)
    )
    halves, group_down = lax.optimization_barrier((halves, group_down))
    outgoing = jnp.broadcast_to(halves[None], (chips, nc, column_width, core_rows))
    core_context = lax.all_to_all(
        outgoing.reshape(group_size, column_width, core_rows), BLK, 0, 0, tiled=True
    ).reshape(group_size * column_width, core_rows)
    chip_width = nc * column_width
    column_bias = lax.dynamic_slice_in_dim(out_biases[0], chip * chip_width, chip_width)
    projected_part = (
        jnp.einsum("ct,cd->dt", core_context, chip_out, preferred_element_type=jnp.float32)
        + column_bias[:, None]
    ).astype(jnp.bfloat16)
    spread = jnp.broadcast_to(projected_part[None], (chips,) + projected_part.shape)
    projected = lax.all_to_all(spread, PLANE, 0, 0, tiled=True).reshape(chips * chip_width, core_rows).T
    core_tokens = lax.dynamic_index_in_dim(
        token_rows.reshape(chips, nc, block_rows, -1), core, axis=1, keepdims=False
    ).reshape(chips * block_rows, -1)
    normed = layer_norm(
        core_tokens.astype(jnp.float32) + projected.astype(jnp.float32),
        norm_gains[0],
        norm_biases[0],
    ).astype(jnp.bfloat16)
    inner = jax.nn.gelu(
        jnp.dot(normed, chip_in, preferred_element_type=jnp.float32) + chip_in_bias, approximate=True
    ).astype(jnp.bfloat16)
    group_inner = lax.all_to_all(
        jnp.broadcast_to(inner[None], (nx,) + inner.shape), "bx", 0, 0, tiled=True
    ).reshape(nx, core_rows, nc, hidden_width)
    mixed_parts = jnp.einsum(
        "xtcf,xcdf->td", group_inner, group_down, preferred_element_type=jnp.float32
    )
    from_chips = lax.all_to_all(
        mixed_parts.reshape(chips, block_rows, quarter_width), PLANE, 0, 0, tiled=True
    ).reshape(nx, ny, block_rows, quarter_width)
    mixed_rows = from_chips.sum(axis=1).transpose(1, 0, 2).reshape(block_rows, d_model)
    own_normed = lax.dynamic_slice_in_dim(normed, chip * block_rows, block_rows, 0)
    layer_output = layer_norm(
        own_normed.astype(jnp.float32) + mixed_rows + out_biases[1], norm_gains[1], norm_biases[1]
    ).astype(jnp.bfloat16)
    return (layer_output[None], appended)


def solution(mesh):
    req, blk = mesh.devices.shape
    fine = Mesh(mesh.devices.reshape(req, 4, blk // 8, 2), ("req",) + BLK)
    return jax.shard_map(
        local,
        mesh=fine,
        in_specs=(
            P("req", None, None),
            P("req", BLK, None, None, None),
            P("req", None),
            P("req"),
            P("req", None),
            P("req", None, BLK),
            P(None, BLK),
            P("req", BLK),
            P("req", BLK),
            P(),
            P("req", BLK),
            P(),
            P(),
            P(),
        ),
        out_specs=(P("req", BLK, None), P("req", None, None, BLK)),
        check_vma=False,
    )
```

```python
import math

import jax
import jax.numpy as jnp
from jax import lax
from jax.sharding import Mesh
from jax.sharding import PartitionSpec as P

HEADS = 16
HEAD_DIM = 128


MASKED = -1e30
PLANE = ("bx", "by")
BLK = ("bx", "by", "bc")


def swap(axis, n):
    return [(i, i ^ 1) for i in range(n)]


def layer_norm(values, gain_row, shift_row):
    centered = values - jnp.mean(values, axis=-1, keepdims=True)
    variance = jnp.mean(centered * centered, axis=-1, keepdims=True)
    return centered * lax.rsqrt(variance + 1e-06) * gain_row + shift_row


def partial_block(queries, key_rows, value_rows, visible):
    scores = jnp.einsum("qd,kd->qk", queries, key_rows, preferred_element_type=jnp.float32) * (
        1.0 / math.sqrt(HEAD_DIM)
    )
    scores = jnp.where(visible, scores, MASKED)
    row_max = jnp.max(scores, axis=1)
    weights = jnp.where(visible, jnp.exp(scores - row_max[:, None]), 0.0)
    row_total = jnp.sum(weights, axis=1)
    numerator = jnp.einsum(
        "qk,kd->dq", weights.astype(jnp.bfloat16), value_rows, preferred_element_type=jnp.float32
    )
    return (numerator, row_max, row_total)


def merge_blocks(earlier_part, later_part):
    joined = jnp.maximum(earlier_part[1], later_part[1])
    scale_earlier = jnp.exp(earlier_part[1] - joined)
    scale_later = jnp.exp(later_part[1] - joined)
    numerator = earlier_part[0] * scale_earlier[:, None] + later_part[0] * scale_later[:, None]
    return (numerator, joined, earlier_part[2] * scale_earlier + later_part[2] * scale_later)


def gather_rows(block):
    reqs = lax.axis_size("req")
    spread = jnp.broadcast_to(block[None], (reqs,) + block.shape)
    return lax.all_to_all(spread, "req", 0, 0, tiled=True).reshape(reqs * block.shape[0], -1)


def core_pair(own, other, core, axis):
    return jnp.where(
        core == 0,
        jnp.concatenate([own, other], axis=axis),
        jnp.concatenate([other, own], axis=axis),
    )


def local(
    tokens,
    cache_entries,
    cache_tenants,
    cached_length,
    tenant_bounds,
    qkv_weight,
    qkv_bias,
    out_weight,
    in_weight,
    in_bias,
    down_weight,
    out_biases,
    norm_gains,
    norm_biases,
):
    nx, ny, nc = lax.axis_size("bx"), lax.axis_size("by"), lax.axis_size("bc")
    core = lax.axis_index("bc")
    chip = lax.axis_index("bx") * ny + lax.axis_index("by")
    block_index = chip * nc + core
    group_size = nx * ny * nc
    groups = group_size // HEADS
    low_bits = groups.bit_length() - 1
    group_index = block_index % groups

    rows, _, column_width = qkv_weight.shape
    qkv_flat = qkv_weight.reshape(rows, 3 * column_width)
    hidden_width = in_weight.shape[1]
    first = gather_rows(jnp.concatenate([qkv_flat, down_weight], axis=1))
    full_qkv = first[:, : 3 * column_width].reshape(-1, 3, column_width)
    d_model = first.shape[0]
    quarter_width = d_model // nx
    own_down = first[:, 3 * column_width :].reshape(nx, 1, quarter_width, hidden_width)
    group_down = lax.all_to_all(
        jnp.broadcast_to(own_down, (nx, nc, quarter_width, hidden_width)).reshape(
            nx * nc, quarter_width, hidden_width
        ),
        ("bx", "bc"),
        0,
        0,
        tiled=True,
    ).reshape(nx, nc, quarter_width, hidden_width)
    packed = jnp.concatenate([out_weight, in_weight], axis=1)
    packed, group_down = lax.optimization_barrier((packed, group_down))
    front = gather_rows(packed)
    sibling = lax.ppermute(front, "bc", swap("bc", nc))
    chip_out = core_pair(front[:, :column_width], sibling[:, :column_width], core, 1)
    chip_in = core_pair(front[:, column_width:], sibling[:, column_width:], core, 1)
    chip_in_bias = lax.dynamic_slice_in_dim(in_bias, chip * nc * hidden_width, nc * hidden_width)

    query_total = tokens.shape[1]
    token_rows = tokens[0]
    qkv_columns = (
        jnp.einsum("td,dce->cet", token_rows, full_qkv, preferred_element_type=jnp.float32)
        + qkv_bias[:, :, None]
    ).astype(jnp.bfloat16)
    appended = qkv_columns[1:].transpose(2, 0, 1)[None]

    def from_partner(value, bit_level):
        if bit_level == 0:
            return lax.ppermute(value, "bc", swap("bc", nc))
        return lax.ppermute(value, "by", [(i, i ^ (1 << (bit_level - 1))) for i in range(ny)])

    head_qkv = qkv_columns
    for bit_level in range(low_bits):
        partner = from_partner(head_qkv, bit_level)
        upper_bit = group_index >> bit_level & 1
        head_qkv = jnp.where(
            upper_bit == 1,
            jnp.concatenate([partner, head_qkv], axis=1),
            jnp.concatenate([head_qkv, partner], axis=1),
        )
    queries = head_qkv[0].T
    fresh_count = query_total // groups
    fresh_start = group_index * fresh_count
    fresh_keys = lax.dynamic_slice_in_dim(head_qkv[1], fresh_start, fresh_count, 1).T
    fresh_values = lax.dynamic_slice_in_dim(head_qkv[2], fresh_start, fresh_count, 1).T
    cache_count = cache_entries.shape[2]
    cache_keys = cache_entries[0, 0, :, 0]
    cache_values = cache_entries[0, 0, :, 1]
    cache_position = group_index * cache_count + jnp.arange(cache_count, dtype=jnp.int32)
    tenant_slice = lax.dynamic_slice_in_dim(
        cache_tenants[0], group_index * cache_count, cache_count, 0
    )
    readable = (
        (cache_position < cached_length[0])
        & (tenant_slice >= tenant_bounds[0, 0])
        & (tenant_slice < tenant_bounds[0, 1])
    )
    query_position = jnp.arange(query_total, dtype=jnp.int32)
    fresh_position = fresh_start + jnp.arange(fresh_count, dtype=jnp.int32)
    fresh_visible = fresh_position[None, :] <= query_position[:, None]
    cache_visible = jnp.broadcast_to(readable[None, :], (query_total, cache_count))
    numerator, row_max, row_total = partial_block(
        queries,
        jnp.concatenate([cache_keys, fresh_keys], axis=0),
        jnp.concatenate([cache_values, fresh_values], axis=0),
        jnp.concatenate([cache_visible, fresh_visible], axis=1),
    )
    for bit_level in reversed(range(low_bits)):
        halves = numerator.reshape(2, -1, query_total)
        upper_bit = group_index >> bit_level & 1
        kept_half = jnp.where(upper_bit == 1, halves[1], halves[0])
        sent_half = jnp.where(upper_bit == 1, halves[0], halves[1])
        sent = jnp.concatenate([sent_half, row_max[None], row_total[None]], axis=0)
        got_back = from_partner(sent, bit_level)
        other_sum, other_max, other_total = got_back[:-2], got_back[-2], got_back[-1]
        joined = jnp.maximum(row_max, other_max)
        scale_kept = jnp.exp(row_max - joined)
        scale_other = jnp.exp(other_max - joined)
        numerator = kept_half * scale_kept[None] + other_sum * scale_other[None]
        row_max, row_total = joined, row_total * scale_kept + other_total * scale_other
    context_columns = (numerator / row_total[None]).astype(jnp.bfloat16)

    block_rows = query_total // (group_size)
    chips = nx * ny
    core_rows = chips * block_rows
    halves = (
        context_columns.reshape(column_width, chips, nc, block_rows)
        .transpose(2, 0, 1, 3)
        .reshape(nc, column_width, core_rows)
    )
    outgoing = jnp.broadcast_to(halves[None], (chips, nc, column_width, core_rows))
    core_context = lax.all_to_all(
        outgoing.reshape(group_size, column_width, core_rows), BLK, 0, 0, tiled=True
    ).reshape(group_size * column_width, core_rows)
    chip_width = nc * column_width
    column_bias = lax.dynamic_slice_in_dim(out_biases[0], chip * chip_width, chip_width)
    projected_part = (
        jnp.einsum("ct,cd->dt", core_context, chip_out, preferred_element_type=jnp.float32)
        + column_bias[:, None]
    ).astype(jnp.bfloat16)
    spread = jnp.broadcast_to(projected_part[None], (chips,) + projected_part.shape)
    projected = lax.all_to_all(spread, PLANE, 0, 0, tiled=True).reshape(chips * chip_width, core_rows).T
    core_tokens = lax.dynamic_index_in_dim(
        token_rows.reshape(chips, nc, block_rows, -1), core, axis=1, keepdims=False
    ).reshape(chips * block_rows, -1)
    normed = layer_norm(
        core_tokens.astype(jnp.float32) + projected.astype(jnp.float32),
        norm_gains[0],
        norm_biases[0],
    ).astype(jnp.bfloat16)
    inner = jax.nn.gelu(
        jnp.dot(normed, chip_in, preferred_element_type=jnp.float32) + chip_in_bias, approximate=True
    ).astype(jnp.bfloat16)
    group_inner = lax.all_to_all(
        jnp.broadcast_to(inner[None], (nx,) + inner.shape), "bx", 0, 0, tiled=True
    ).reshape(nx, core_rows, nc, hidden_width)
    mixed_parts = jnp.einsum(
        "xtcf,xcdf->td", group_inner, group_down, preferred_element_type=jnp.float32
    )
    from_chips = lax.all_to_all(
        mixed_parts.reshape(chips, block_rows, quarter_width), PLANE, 0, 0, tiled=True
    ).reshape(nx, ny, block_rows, quarter_width)
    mixed_rows = from_chips.sum(axis=1).transpose(1, 0, 2).reshape(block_rows, d_model)
    own_normed = lax.dynamic_slice_in_dim(normed, chip * block_rows, block_rows, 0)
    layer_output = layer_norm(
        own_normed.astype(jnp.float32) + mixed_rows + out_biases[1], norm_gains[1], norm_biases[1]
    ).astype(jnp.bfloat16)
    return (layer_output[None], appended)


def solution(mesh):
    req, blk = mesh.devices.shape
    fine = Mesh(mesh.devices.reshape(req, 4, blk // 8, 2), ("req",) + BLK)
    return jax.shard_map(
        local,
        mesh=fine,
        in_specs=(
            P("req", None, None),
            P("req", BLK, None, None, None),
            P("req", None),
            P("req"),
            P("req", None),
            P("req", None, BLK),
            P(None, BLK),
            P("req", BLK),
            P("req", BLK),
            P(),
            P("req", BLK),
            P(),
            P(),
            P(),
        ),
        out_specs=(P("req", BLK, None), P("req", None, None, BLK)),
        check_vma=False,
    )
```

```python
import math

import jax
import jax.numpy as jnp
from jax import lax
from jax.sharding import Mesh
from jax.sharding import PartitionSpec as P

HEADS = 16
HEAD_DIM = 128


MASKED = -1e30
PLANE = ("bx", "by")
BLK = ("bx", "by", "bc")


def swap(axis, n):
    return [(i, i ^ 1) for i in range(n)]


def layer_norm(values, gain_row, shift_row):
    centered = values - jnp.mean(values, axis=-1, keepdims=True)
    variance = jnp.mean(centered * centered, axis=-1, keepdims=True)
    return centered * lax.rsqrt(variance + 1e-06) * gain_row + shift_row


def partial_block(queries, key_rows, value_rows, visible):
    scores = jnp.einsum("qd,kd->qk", queries, key_rows, preferred_element_type=jnp.float32) * (
        1.0 / math.sqrt(HEAD_DIM)
    )
    scores = jnp.where(visible, scores, MASKED)
    row_max = jnp.max(scores, axis=1)
    weights = jnp.where(visible, jnp.exp(scores - row_max[:, None]), 0.0)
    row_total = jnp.sum(weights, axis=1)
    numerator = jnp.einsum(
        "qk,kd->dq", weights.astype(jnp.bfloat16), value_rows, preferred_element_type=jnp.float32
    )
    return (numerator, row_max, row_total)


def merge_blocks(earlier_part, later_part):
    joined = jnp.maximum(earlier_part[1], later_part[1])
    scale_earlier = jnp.exp(earlier_part[1] - joined)
    scale_later = jnp.exp(later_part[1] - joined)
    numerator = earlier_part[0] * scale_earlier[:, None] + later_part[0] * scale_later[:, None]
    return (numerator, joined, earlier_part[2] * scale_earlier + later_part[2] * scale_later)


def gather_rows(block):
    reqs = lax.axis_size("req")
    spread = jnp.broadcast_to(block[None], (reqs,) + block.shape)
    return lax.all_to_all(spread, "req", 0, 0, tiled=True).reshape(reqs * block.shape[0], -1)


def core_pair(own, other, core, axis):
    return jnp.where(
        core == 0,
        jnp.concatenate([own, other], axis=axis),
        jnp.concatenate([other, own], axis=axis),
    )


def local(
    tokens,
    cache_entries,
    cache_tenants,
    cached_length,
    tenant_bounds,
    qkv_weight,
    qkv_bias,
    out_weight,
    in_weight,
    in_bias,
    down_weight,
    out_biases,
    norm_gains,
    norm_biases,
):
    nx, ny, nc = lax.axis_size("bx"), lax.axis_size("by"), lax.axis_size("bc")
    core = lax.axis_index("bc")
    chip = lax.axis_index("bx") * ny + lax.axis_index("by")
    block_index = chip * nc + core
    group_size = nx * ny * nc
    groups = group_size // HEADS
    low_bits = groups.bit_length() - 1
    group_index = block_index % groups

    rows, _, column_width = qkv_weight.shape
    qkv_flat = qkv_weight.reshape(rows, 3 * column_width)
    hidden_width = in_weight.shape[1]
    packed = jnp.concatenate([out_weight, in_weight, down_weight], axis=1)
    full_qkv = gather_rows(qkv_flat).reshape(-1, 3, column_width)
    late = gather_rows(packed)
    front = late[:, : column_width + hidden_width]
    sibling = lax.ppermute(front, "bc", swap("bc", nc))
    chip_out = core_pair(front[:, :column_width], sibling[:, :column_width], core, 1)
    chip_in = core_pair(front[:, column_width:], sibling[:, column_width:], core, 1)
    chip_in_bias = lax.dynamic_slice_in_dim(in_bias, chip * nc * hidden_width, nc * hidden_width)
    d_model = late.shape[0]
    quarter_width = d_model // nx
    own_down = late[:, column_width + hidden_width :].reshape(nx, quarter_width, hidden_width)
    from_row = lax.all_to_all(own_down, "bx", 0, 0, tiled=True)
    from_sibling = lax.ppermute(from_row, "bc", swap("bc", nc))
    group_down = core_pair(from_row[:, None], from_sibling[:, None], core, 1)

    query_total = tokens.shape[1]
    token_rows = tokens[0]
    qkv_columns = (
        jnp.einsum("td,dce->cet", token_rows, full_qkv, preferred_element_type=jnp.float32)
        + qkv_bias[:, :, None]
    ).astype(jnp.bfloat16)
    appended = qkv_columns[1:].transpose(2, 0, 1)[None]

    def from_partner(value, bit_level):
        if bit_level == 0:
            return lax.ppermute(value, "bc", swap("bc", nc))
        return lax.ppermute(value, "by", [(i, i ^ (1 << (bit_level - 1))) for i in range(ny)])

    head_qkv = qkv_columns
    for bit_level in range(low_bits):
        partner = from_partner(head_qkv, bit_level)
        upper_bit = group_index >> bit_level & 1
        head_qkv = jnp.where(
            upper_bit == 1,
            jnp.concatenate([partner, head_qkv], axis=1),
            jnp.concatenate([head_qkv, partner], axis=1),
        )
    queries = head_qkv[0].T
    fresh_count = query_total // groups
    fresh_start = group_index * fresh_count
    fresh_keys = lax.dynamic_slice_in_dim(head_qkv[1], fresh_start, fresh_count, 1).T
    fresh_values = lax.dynamic_slice_in_dim(head_qkv[2], fresh_start, fresh_count, 1).T
    cache_count = cache_entries.shape[2]
    cache_keys = cache_entries[0, 0, :, 0]
    cache_values = cache_entries[0, 0, :, 1]
    cache_position = group_index * cache_count + jnp.arange(cache_count, dtype=jnp.int32)
    tenant_slice = lax.dynamic_slice_in_dim(
        cache_tenants[0], group_index * cache_count, cache_count, 0
    )
    readable = (
        (cache_position < cached_length[0])
        & (tenant_slice >= tenant_bounds[0, 0])
        & (tenant_slice < tenant_bounds[0, 1])
    )
    query_position = jnp.arange(query_total, dtype=jnp.int32)
    fresh_position = fresh_start + jnp.arange(fresh_count, dtype=jnp.int32)
    fresh_visible = fresh_position[None, :] <= query_position[:, None]
    cache_visible = jnp.broadcast_to(readable[None, :], (query_total, cache_count))
    numerator, row_max, row_total = partial_block(
        queries,
        jnp.concatenate([cache_keys, fresh_keys], axis=0),
        jnp.concatenate([cache_values, fresh_values], axis=0),
        jnp.concatenate([cache_visible, fresh_visible], axis=1),
    )
    for bit_level in reversed(range(low_bits)):
        halves = numerator.reshape(2, -1, query_total)
        upper_bit = group_index >> bit_level & 1
        kept_half = jnp.where(upper_bit == 1, halves[1], halves[0])
        sent_half = jnp.where(upper_bit == 1, halves[0], halves[1])
        sent = jnp.concatenate([sent_half, row_max[None], row_total[None]], axis=0)
        got_back = from_partner(sent, bit_level)
        other_sum, other_max, other_total = got_back[:-2], got_back[-2], got_back[-1]
        joined = jnp.maximum(row_max, other_max)
        scale_kept = jnp.exp(row_max - joined)
        scale_other = jnp.exp(other_max - joined)
        numerator = kept_half * scale_kept[None] + other_sum * scale_other[None]
        row_max, row_total = joined, row_total * scale_kept + other_total * scale_other
    context_columns = (numerator / row_total[None]).astype(jnp.bfloat16)

    block_rows = query_total // (group_size)
    chips = nx * ny
    core_rows = chips * block_rows
    halves = (
        context_columns.reshape(column_width, chips, nc, block_rows)
        .transpose(2, 0, 1, 3)
        .reshape(nc, column_width, core_rows)
    )
    halves, group_down = lax.optimization_barrier((halves, group_down))
    outgoing = jnp.broadcast_to(halves[None], (chips, nc, column_width, core_rows))
    core_context = lax.all_to_all(
        outgoing.reshape(group_size, column_width, core_rows), BLK, 0, 0, tiled=True
    ).reshape(group_size * column_width, core_rows)
    chip_width = nc * column_width
    column_bias = lax.dynamic_slice_in_dim(out_biases[0], chip * chip_width, chip_width)
    projected_part = (
        jnp.einsum("ct,cd->dt", core_context, chip_out, preferred_element_type=jnp.float32)
        + column_bias[:, None]
    ).astype(jnp.bfloat16)
    spread = jnp.broadcast_to(projected_part[None], (chips,) + projected_part.shape)
    projected = lax.all_to_all(spread, PLANE, 0, 0, tiled=True).reshape(chips * chip_width, core_rows)
    core_tokens = lax.dynamic_index_in_dim(
        token_rows.reshape(chips, nc, block_rows, -1), core, axis=1, keepdims=False
    ).reshape(core_rows, -1)
    residual = core_tokens.T.astype(jnp.float32) + projected.astype(jnp.float32)
    centered = residual - jnp.mean(residual, axis=0, keepdims=True)
    variance = jnp.mean(centered * centered, axis=0, keepdims=True)
    normed_t = (
        centered * lax.rsqrt(variance + 1e-06) * norm_gains[0][:, None] + norm_biases[0][:, None]
    ).astype(jnp.bfloat16)
    inner = jax.nn.gelu(
        jnp.einsum("dt,df->tf", normed_t, chip_in, preferred_element_type=jnp.float32) + chip_in_bias,
        approximate=True,
    ).astype(jnp.bfloat16)
    group_inner = lax.all_to_all(
        jnp.broadcast_to(inner[None], (nx,) + inner.shape), "bx", 0, 0, tiled=True
    ).reshape(nx, core_rows, nc, hidden_width)
    mixed_parts = jnp.einsum(
        "xtcf,xcdf->td", group_inner, group_down, preferred_element_type=jnp.float32
    )
    from_chips = lax.all_to_all(
        mixed_parts.reshape(chips, block_rows, quarter_width), PLANE, 0, 0, tiled=True
    ).reshape(nx, ny, block_rows, quarter_width)
    mixed_rows = from_chips.sum(axis=1).transpose(1, 0, 2).reshape(block_rows, d_model)
    own_normed = lax.dynamic_slice_in_dim(normed_t, chip * block_rows, block_rows, 1).T
    layer_output = layer_norm(
        own_normed.astype(jnp.float32) + mixed_rows + out_biases[1], norm_gains[1], norm_biases[1]
    ).astype(jnp.bfloat16)
    return (layer_output[None], appended)


def solution(mesh):
    req, blk = mesh.devices.shape
    fine = Mesh(mesh.devices.reshape(req, 4, blk // 8, 2), ("req",) + BLK)
    return jax.shard_map(
        local,
        mesh=fine,
        in_specs=(
            P("req", None, None),
            P("req", BLK, None, None, None),
            P("req", None),
            P("req"),
            P("req", None),
            P("req", None, BLK),
            P(None, BLK),
            P("req", BLK),
            P("req", BLK),
            P(),
            P("req", BLK),
            P(),
            P(),
            P(),
        ),
        out_specs=(P("req", BLK, None), P("req", None, None, BLK)),
        check_vma=False,
    )
```

```python
import math

import jax
import jax.numpy as jnp
from jax import lax
from jax.sharding import Mesh
from jax.sharding import PartitionSpec as P

HEADS = 16
HEAD_DIM = 128


MASKED = -1e30
PLANE = ("bx", "by")
BLK = ("bx", "by", "bc")


def swap(axis, n):
    return [(i, i ^ 1) for i in range(n)]


def layer_norm(values, gain_row, shift_row):
    centered = values - jnp.mean(values, axis=-1, keepdims=True)
    variance = jnp.mean(centered * centered, axis=-1, keepdims=True)
    return centered * lax.rsqrt(variance + 1e-06) * gain_row + shift_row


def partial_block(queries, key_rows, value_rows, visible):
    scores = jnp.einsum("qd,kd->qk", queries, key_rows, preferred_element_type=jnp.float32) * (
        1.0 / math.sqrt(HEAD_DIM)
    )
    scores = jnp.where(visible, scores, MASKED)
    row_max = jnp.max(scores, axis=1)
    weights = jnp.where(visible, jnp.exp(scores - row_max[:, None]), 0.0)
    row_total = jnp.sum(weights, axis=1)
    numerator = jnp.einsum(
        "qk,kd->dq", weights.astype(jnp.bfloat16), value_rows, preferred_element_type=jnp.float32
    )
    return (numerator, row_max, row_total)


def merge_blocks(earlier_part, later_part):
    joined = jnp.maximum(earlier_part[1], later_part[1])
    scale_earlier = jnp.exp(earlier_part[1] - joined)
    scale_later = jnp.exp(later_part[1] - joined)
    numerator = earlier_part[0] * scale_earlier[:, None] + later_part[0] * scale_later[:, None]
    return (numerator, joined, earlier_part[2] * scale_earlier + later_part[2] * scale_later)


def gather_rows(block):
    reqs = lax.axis_size("req")
    spread = jnp.broadcast_to(block[None], (reqs,) + block.shape)
    return lax.all_to_all(spread, "req", 0, 0, tiled=True).reshape(reqs * block.shape[0], -1)


def core_pair(own, other, core, axis):
    return jnp.where(
        core == 0,
        jnp.concatenate([own, other], axis=axis),
        jnp.concatenate([other, own], axis=axis),
    )


def local(
    tokens,
    cache_entries,
    cache_tenants,
    cached_length,
    tenant_bounds,
    qkv_weight,
    qkv_bias,
    out_weight,
    in_weight,
    in_bias,
    down_weight,
    out_biases,
    norm_gains,
    norm_biases,
):
    nx, ny, nc = lax.axis_size("bx"), lax.axis_size("by"), lax.axis_size("bc")
    core = lax.axis_index("bc")
    chip = lax.axis_index("bx") * ny + lax.axis_index("by")
    block_index = chip * nc + core
    group_size = nx * ny * nc
    groups = group_size // HEADS
    low_bits = groups.bit_length() - 1
    group_index = block_index % groups

    rows, _, column_width = qkv_weight.shape
    qkv_flat = qkv_weight.reshape(rows, 3 * column_width)
    hidden_width = in_weight.shape[1]
    packed = jnp.concatenate([out_weight, in_weight, down_weight], axis=1)
    full_qkv = gather_rows(qkv_flat).reshape(-1, 3, column_width)
    late = gather_rows(packed)
    front = late[:, : column_width + hidden_width]
    sibling = lax.ppermute(front, "bc", swap("bc", nc))
    chip_out = core_pair(front[:, :column_width], sibling[:, :column_width], core, 1)
    chip_in = core_pair(front[:, column_width:], sibling[:, column_width:], core, 1)
    chip_in_bias = lax.dynamic_slice_in_dim(in_bias, chip * nc * hidden_width, nc * hidden_width)
    d_model = late.shape[0]
    quarter_width = d_model // nx
    own_down = late[:, column_width + hidden_width :].reshape(nx, quarter_width, hidden_width)
    row = lax.axis_index("bx")
    received = [lax.dynamic_index_in_dim(own_down, row, 0, keepdims=False)]
    for k in range(1, nx):
        received.append(
            lax.ppermute(
                lax.dynamic_index_in_dim(own_down, row ^ k, 0, keepdims=False),
                "bx",
                [(i, i ^ k) for i in range(nx)],
            )
        )
    from_row = jnp.take(jnp.stack(received), row ^ jnp.arange(nx), axis=0)
    from_sibling = lax.ppermute(from_row, "bc", swap("bc", nc))
    group_down = core_pair(from_row[:, None], from_sibling[:, None], core, 1)

    query_total = tokens.shape[1]
    token_rows = tokens[0]
    qkv_columns = (
        jnp.einsum("td,dce->cet", token_rows, full_qkv, preferred_element_type=jnp.float32)
        + qkv_bias[:, :, None]
    ).astype(jnp.bfloat16)
    appended = qkv_columns[1:].transpose(2, 0, 1)[None]

    def from_partner(value, bit_level):
        if bit_level == 0:
            return lax.ppermute(value, "bc", swap("bc", nc))
        return lax.ppermute(value, "by", [(i, i ^ (1 << (bit_level - 1))) for i in range(ny)])

    head_qkv = qkv_columns
    for bit_level in range(low_bits):
        partner = from_partner(head_qkv, bit_level)
        upper_bit = group_index >> bit_level & 1
        head_qkv = jnp.where(
            upper_bit == 1,
            jnp.concatenate([partner, head_qkv], axis=1),
            jnp.concatenate([head_qkv, partner], axis=1),
        )
    queries = head_qkv[0].T
    fresh_count = query_total // groups
    fresh_start = group_index * fresh_count
    fresh_keys = lax.dynamic_slice_in_dim(head_qkv[1], fresh_start, fresh_count, 1).T
    fresh_values = lax.dynamic_slice_in_dim(head_qkv[2], fresh_start, fresh_count, 1).T
    cache_count = cache_entries.shape[2]
    cache_keys = cache_entries[0, 0, :, 0]
    cache_values = cache_entries[0, 0, :, 1]
    cache_position = group_index * cache_count + jnp.arange(cache_count, dtype=jnp.int32)
    tenant_slice = lax.dynamic_slice_in_dim(
        cache_tenants[0], group_index * cache_count, cache_count, 0
    )
    readable = (
        (cache_position < cached_length[0])
        & (tenant_slice >= tenant_bounds[0, 0])
        & (tenant_slice < tenant_bounds[0, 1])
    )
    query_position = jnp.arange(query_total, dtype=jnp.int32)
    fresh_position = fresh_start + jnp.arange(fresh_count, dtype=jnp.int32)
    fresh_visible = fresh_position[None, :] <= query_position[:, None]
    cache_visible = jnp.broadcast_to(readable[None, :], (query_total, cache_count))
    numerator, row_max, row_total = partial_block(
        queries,
        jnp.concatenate([cache_keys, fresh_keys], axis=0),
        jnp.concatenate([cache_values, fresh_values], axis=0),
        jnp.concatenate([cache_visible, fresh_visible], axis=1),
    )
    for bit_level in reversed(range(low_bits)):
        halves = numerator.reshape(2, -1, query_total)
        upper_bit = group_index >> bit_level & 1
        kept_half = jnp.where(upper_bit == 1, halves[1], halves[0])
        sent_half = jnp.where(upper_bit == 1, halves[0], halves[1])
        sent = jnp.concatenate([sent_half, row_max[None], row_total[None]], axis=0)
        got_back = from_partner(sent, bit_level)
        other_sum, other_max, other_total = got_back[:-2], got_back[-2], got_back[-1]
        joined = jnp.maximum(row_max, other_max)
        scale_kept = jnp.exp(row_max - joined)
        scale_other = jnp.exp(other_max - joined)
        numerator = kept_half * scale_kept[None] + other_sum * scale_other[None]
        row_max, row_total = joined, row_total * scale_kept + other_total * scale_other
    context_columns = (numerator / row_total[None]).astype(jnp.bfloat16)

    block_rows = query_total // (group_size)
    chips = nx * ny
    core_rows = chips * block_rows
    halves = (
        context_columns.reshape(column_width, chips, nc, block_rows)
        .transpose(2, 0, 1, 3)
        .reshape(nc, column_width, core_rows)
    )
    outgoing = jnp.broadcast_to(halves[None], (chips, nc, column_width, core_rows))
    core_context = lax.all_to_all(
        outgoing.reshape(group_size, column_width, core_rows), BLK, 0, 0, tiled=True
    ).reshape(group_size * column_width, core_rows)
    chip_width = nc * column_width
    column_bias = lax.dynamic_slice_in_dim(out_biases[0], chip * chip_width, chip_width)
    projected_part = (
        jnp.einsum("ct,cd->dt", core_context, chip_out, preferred_element_type=jnp.float32)
        + column_bias[:, None]
    ).astype(jnp.bfloat16)
    spread = jnp.broadcast_to(projected_part[None], (chips,) + projected_part.shape)
    spread, group_down = lax.optimization_barrier((spread, group_down))
    projected = lax.all_to_all(spread, PLANE, 0, 0, tiled=True).reshape(chips * chip_width, core_rows)
    core_tokens = lax.dynamic_index_in_dim(
        token_rows.reshape(chips, nc, block_rows, -1), core, axis=1, keepdims=False
    ).reshape(core_rows, -1)
    residual = core_tokens.T.astype(jnp.float32) + projected.astype(jnp.float32)
    centered = residual - jnp.mean(residual, axis=0, keepdims=True)
    variance = jnp.mean(centered * centered, axis=0, keepdims=True)
    normed_t = (
        centered * lax.rsqrt(variance + 1e-06) * norm_gains[0][:, None] + norm_biases[0][:, None]
    ).astype(jnp.bfloat16)
    inner = jax.nn.gelu(
        jnp.einsum("dt,df->tf", normed_t, chip_in, preferred_element_type=jnp.float32) + chip_in_bias,
        approximate=True,
    ).astype(jnp.bfloat16)
    group_inner = lax.all_to_all(
        jnp.broadcast_to(inner[None], (nx,) + inner.shape), "bx", 0, 0, tiled=True
    ).reshape(nx, core_rows, nc, hidden_width)
    mixed_parts = jnp.einsum(
        "xtcf,xcdf->td", group_inner, group_down, preferred_element_type=jnp.float32
    )
    from_chips = lax.all_to_all(
        mixed_parts.reshape(chips, block_rows, quarter_width), PLANE, 0, 0, tiled=True
    ).reshape(nx, ny, block_rows, quarter_width)
    mixed_rows = from_chips.sum(axis=1).transpose(1, 0, 2).reshape(block_rows, d_model)
    own_normed = lax.dynamic_slice_in_dim(normed_t, chip * block_rows, block_rows, 1).T
    layer_output = layer_norm(
        own_normed.astype(jnp.float32) + mixed_rows + out_biases[1], norm_gains[1], norm_biases[1]
    ).astype(jnp.bfloat16)
    return (layer_output[None], appended)


def solution(mesh):
    req, blk = mesh.devices.shape
    fine = Mesh(mesh.devices.reshape(req, 4, blk // 8, 2), ("req",) + BLK)
    return jax.shard_map(
        local,
        mesh=fine,
        in_specs=(
            P("req", None, None),
            P("req", BLK, None, None, None),
            P("req", None),
            P("req"),
            P("req", None),
            P("req", None, BLK),
            P(None, BLK),
            P("req", BLK),
            P("req", BLK),
            P(),
            P("req", BLK),
            P(),
            P(),
            P(),
        ),
        out_specs=(P("req", BLK, None), P("req", None, None, BLK)),
        check_vma=False,
    )
```

```python
import math

import jax
import jax.numpy as jnp
from jax import lax
from jax.sharding import Mesh
from jax.sharding import PartitionSpec as P

HEADS = 16
HEAD_DIM = 128


MASKED = -1e30
PLANE = ("bx", "by")
BLK = ("bx", "by", "bc")


def swap(axis, n):
    return [(i, i ^ 1) for i in range(n)]


def layer_norm(values, gain_row, shift_row):
    centered = values - jnp.mean(values, axis=-1, keepdims=True)
    variance = jnp.mean(centered * centered, axis=-1, keepdims=True)
    return centered * lax.rsqrt(variance + 1e-06) * gain_row + shift_row


def partial_block(queries, key_rows, value_rows, visible):
    scores = jnp.einsum("qd,kd->qk", queries, key_rows, preferred_element_type=jnp.float32) * (
        1.0 / math.sqrt(HEAD_DIM)
    )
    scores = jnp.where(visible, scores, MASKED)
    row_max = jnp.max(scores, axis=1)
    weights = jnp.where(visible, jnp.exp(scores - row_max[:, None]), 0.0)
    row_total = jnp.sum(weights, axis=1)
    numerator = jnp.einsum(
        "qk,kd->dq", weights.astype(jnp.bfloat16), value_rows, preferred_element_type=jnp.float32
    )
    return (numerator, row_max, row_total)


def merge_blocks(earlier_part, later_part):
    joined = jnp.maximum(earlier_part[1], later_part[1])
    scale_earlier = jnp.exp(earlier_part[1] - joined)
    scale_later = jnp.exp(later_part[1] - joined)
    numerator = earlier_part[0] * scale_earlier[:, None] + later_part[0] * scale_later[:, None]
    return (numerator, joined, earlier_part[2] * scale_earlier + later_part[2] * scale_later)


def gather_rows(block):
    reqs = lax.axis_size("req")
    spread = jnp.broadcast_to(block[None], (reqs,) + block.shape)
    return lax.all_to_all(spread, "req", 0, 0, tiled=True).reshape(reqs * block.shape[0], -1)


def core_pair(own, other, core, axis):
    return jnp.where(
        core == 0,
        jnp.concatenate([own, other], axis=axis),
        jnp.concatenate([other, own], axis=axis),
    )


def local(
    tokens,
    cache_entries,
    cache_tenants,
    cached_length,
    tenant_bounds,
    qkv_weight,
    qkv_bias,
    out_weight,
    in_weight,
    in_bias,
    down_weight,
    out_biases,
    norm_gains,
    norm_biases,
):
    nx, ny, nc = lax.axis_size("bx"), lax.axis_size("by"), lax.axis_size("bc")
    core = lax.axis_index("bc")
    chip = lax.axis_index("bx") * ny + lax.axis_index("by")
    block_index = chip * nc + core
    group_size = nx * ny * nc
    groups = group_size // HEADS
    low_bits = groups.bit_length() - 1
    group_index = block_index % groups

    rows, _, column_width = qkv_weight.shape
    qkv_flat = qkv_weight.reshape(rows, 3 * column_width)
    hidden_width = in_weight.shape[1]
    packed = jnp.concatenate([out_weight, in_weight, down_weight], axis=1)
    reqs = lax.axis_size("req")
    qkv_blocks = lax.all_to_all(
        jnp.broadcast_to(qkv_flat[None], (reqs,) + qkv_flat.shape), "req", 0, 0, tiled=True
    ).reshape(reqs, rows, 3, column_width)
    late = gather_rows(packed)
    front = late[:, : column_width + hidden_width]
    sibling = lax.ppermute(front, "bc", swap("bc", nc))
    chip_out = core_pair(front[:, :column_width], sibling[:, :column_width], core, 1)
    chip_in = core_pair(front[:, column_width:], sibling[:, column_width:], core, 1)
    chip_in_bias = lax.dynamic_slice_in_dim(in_bias, chip * nc * hidden_width, nc * hidden_width)
    d_model = late.shape[0]
    quarter_width = d_model // nx
    own_down = late[:, column_width + hidden_width :].reshape(nx, quarter_width, hidden_width)
    row = lax.axis_index("bx")
    received = [lax.dynamic_index_in_dim(own_down, row, 0, keepdims=False)]
    for k in range(1, nx):
        received.append(
            lax.ppermute(
                lax.dynamic_index_in_dim(own_down, row ^ k, 0, keepdims=False),
                "bx",
                [(i, i ^ k) for i in range(nx)],
            )
        )
    from_row = jnp.take(jnp.stack(received), row ^ jnp.arange(nx), axis=0)
    from_sibling = lax.ppermute(from_row, "bc", swap("bc", nc))
    group_down = core_pair(from_row[:, None], from_sibling[:, None], core, 1)

    query_total = tokens.shape[1]
    token_rows = tokens[0]
    qkv_columns = (
        jnp.einsum(
            "tsd,sdce->cet",
            token_rows.reshape(query_total, reqs, rows),
            qkv_blocks,
            preferred_element_type=jnp.float32,
        )
        + qkv_bias[:, :, None]
    ).astype(jnp.bfloat16)
    appended = qkv_columns[1:].transpose(2, 0, 1)[None]

    def from_partner(value, bit_level):
        if bit_level == 0:
            return lax.ppermute(value, "bc", swap("bc", nc))
        return lax.ppermute(value, "by", [(i, i ^ (1 << (bit_level - 1))) for i in range(ny)])

    head_qkv = qkv_columns
    for bit_level in range(low_bits):
        partner = from_partner(head_qkv, bit_level)
        upper_bit = group_index >> bit_level & 1
        head_qkv = jnp.where(
            upper_bit == 1,
            jnp.concatenate([partner, head_qkv], axis=1),
            jnp.concatenate([head_qkv, partner], axis=1),
        )
    queries = head_qkv[0].T
    fresh_count = query_total // groups
    fresh_start = group_index * fresh_count
    fresh_keys = lax.dynamic_slice_in_dim(head_qkv[1], fresh_start, fresh_count, 1).T
    fresh_values = lax.dynamic_slice_in_dim(head_qkv[2], fresh_start, fresh_count, 1).T
    cache_count = cache_entries.shape[2]
    cache_keys = cache_entries[0, 0, :, 0]
    cache_values = cache_entries[0, 0, :, 1]
    cache_position = group_index * cache_count + jnp.arange(cache_count, dtype=jnp.int32)
    tenant_slice = lax.dynamic_slice_in_dim(
        cache_tenants[0], group_index * cache_count, cache_count, 0
    )
    readable = (
        (cache_position < cached_length[0])
        & (tenant_slice >= tenant_bounds[0, 0])
        & (tenant_slice < tenant_bounds[0, 1])
    )
    query_position = jnp.arange(query_total, dtype=jnp.int32)
    fresh_position = fresh_start + jnp.arange(fresh_count, dtype=jnp.int32)
    fresh_visible = fresh_position[None, :] <= query_position[:, None]
    cache_visible = jnp.broadcast_to(readable[None, :], (query_total, cache_count))
    numerator, row_max, row_total = partial_block(
        queries,
        jnp.concatenate([cache_keys, fresh_keys], axis=0),
        jnp.concatenate([cache_values, fresh_values], axis=0),
        jnp.concatenate([cache_visible, fresh_visible], axis=1),
    )
    for bit_level in reversed(range(low_bits)):
        halves = numerator.reshape(2, -1, query_total)
        upper_bit = group_index >> bit_level & 1
        kept_half = jnp.where(upper_bit == 1, halves[1], halves[0])
        sent_half = jnp.where(upper_bit == 1, halves[0], halves[1])
        sent = jnp.concatenate([sent_half, row_max[None], row_total[None]], axis=0)
        got_back = from_partner(sent, bit_level)
        other_sum, other_max, other_total = got_back[:-2], got_back[-2], got_back[-1]
        joined = jnp.maximum(row_max, other_max)
        scale_kept = jnp.exp(row_max - joined)
        scale_other = jnp.exp(other_max - joined)
        numerator = kept_half * scale_kept[None] + other_sum * scale_other[None]
        row_max, row_total = joined, row_total * scale_kept + other_total * scale_other
    context_columns = (numerator / row_total[None]).astype(jnp.bfloat16)

    block_rows = query_total // (group_size)
    chips = nx * ny
    core_rows = chips * block_rows
    halves = (
        context_columns.reshape(column_width, chips, nc, block_rows)
        .transpose(2, 0, 1, 3)
        .reshape(nc, column_width, core_rows)
    )
    outgoing = jnp.broadcast_to(halves[None], (chips, nc, column_width, core_rows))
    core_context = lax.all_to_all(
        outgoing.reshape(group_size, column_width, core_rows), BLK, 0, 0, tiled=True
    ).reshape(group_size * column_width, core_rows)
    chip_width = nc * column_width
    column_bias = lax.dynamic_slice_in_dim(out_biases[0], chip * chip_width, chip_width)
    projected_part = (
        jnp.einsum("ct,cd->dt", core_context, chip_out, preferred_element_type=jnp.float32)
        + column_bias[:, None]
    ).astype(jnp.bfloat16)
    spread = jnp.broadcast_to(projected_part[None], (chips,) + projected_part.shape)
    spread, group_down = lax.optimization_barrier((spread, group_down))
    projected = lax.all_to_all(spread, PLANE, 0, 0, tiled=True).reshape(chips * chip_width, core_rows)
    core_tokens = lax.dynamic_index_in_dim(
        token_rows.reshape(chips, nc, block_rows, -1), core, axis=1, keepdims=False
    ).reshape(core_rows, -1)
    residual = core_tokens.T.astype(jnp.float32) + projected.astype(jnp.float32)
    centered = residual - jnp.mean(residual, axis=0, keepdims=True)
    variance = jnp.mean(centered * centered, axis=0, keepdims=True)
    normed_t = (
        centered * lax.rsqrt(variance + 1e-06) * norm_gains[0][:, None] + norm_biases[0][:, None]
    ).astype(jnp.bfloat16)
    inner = jax.nn.gelu(
        jnp.einsum("dt,df->tf", normed_t, chip_in, preferred_element_type=jnp.float32) + chip_in_bias,
        approximate=True,
    ).astype(jnp.bfloat16)
    group_inner = lax.all_to_all(
        jnp.broadcast_to(inner[None], (nx,) + inner.shape), "bx", 0, 0, tiled=True
    ).reshape(nx, core_rows, nc, hidden_width)
    mixed_parts = jnp.einsum(
        "xtcf,xcdf->td", group_inner, group_down, preferred_element_type=jnp.float32
    )
    from_chips = lax.all_to_all(
        mixed_parts.reshape(chips, block_rows, quarter_width), PLANE, 0, 0, tiled=True
    ).reshape(nx, ny, block_rows, quarter_width)
    mixed_rows = from_chips.sum(axis=1).transpose(1, 0, 2).reshape(block_rows, d_model)
    own_normed = lax.dynamic_slice_in_dim(normed_t, chip * block_rows, block_rows, 1).T
    layer_output = layer_norm(
        own_normed.astype(jnp.float32) + mixed_rows + out_biases[1], norm_gains[1], norm_biases[1]
    ).astype(jnp.bfloat16)
    return (layer_output[None], appended)


def solution(mesh):
    req, blk = mesh.devices.shape
    fine = Mesh(mesh.devices.reshape(req, 4, blk // 8, 2), ("req",) + BLK)
    return jax.shard_map(
        local,
        mesh=fine,
        in_specs=(
            P("req", None, None),
            P("req", BLK, None, None, None),
            P("req", None),
            P("req"),
            P("req", None),
            P("req", None, BLK),
            P(None, BLK),
            P("req", BLK),
            P("req", BLK),
            P(),
            P("req", BLK),
            P(),
            P(),
            P(),
        ),
        out_specs=(P("req", BLK, None), P("req", None, None, BLK)),
        check_vma=False,
    )
```

```python
import math

import jax
import jax.numpy as jnp
from jax import lax
from jax.sharding import Mesh
from jax.sharding import PartitionSpec as P

HEADS = 16
HEAD_DIM = 128


MASKED = -1e30
PLANE = ("bx", "by")
BLK = ("bx", "by", "bc")


def swap(axis, n):
    return [(i, i ^ 1) for i in range(n)]


def layer_norm(values, gain_row, shift_row):
    centered = values - jnp.mean(values, axis=-1, keepdims=True)
    variance = jnp.mean(centered * centered, axis=-1, keepdims=True)
    return centered * lax.rsqrt(variance + 1e-06) * gain_row + shift_row


def partial_block(queries, key_rows, value_rows, visible):
    scores = jnp.einsum("qd,kd->qk", queries, key_rows, preferred_element_type=jnp.float32) * (
        1.0 / math.sqrt(HEAD_DIM)
    )
    scores = jnp.where(visible, scores, MASKED)
    row_max = jnp.max(scores, axis=1)
    weights = jnp.where(visible, jnp.exp(scores - row_max[:, None]), 0.0)
    row_total = jnp.sum(weights, axis=1)
    numerator = jnp.einsum(
        "qk,kd->dq", weights.astype(jnp.bfloat16), value_rows, preferred_element_type=jnp.float32
    )
    return (numerator, row_max, row_total)


def merge_blocks(earlier_part, later_part):
    joined = jnp.maximum(earlier_part[1], later_part[1])
    scale_earlier = jnp.exp(earlier_part[1] - joined)
    scale_later = jnp.exp(later_part[1] - joined)
    numerator = earlier_part[0] * scale_earlier[:, None] + later_part[0] * scale_later[:, None]
    return (numerator, joined, earlier_part[2] * scale_earlier + later_part[2] * scale_later)


def gather_rows(block):
    reqs = lax.axis_size("req")
    spread = jnp.broadcast_to(block[None], (reqs,) + block.shape)
    return lax.all_to_all(spread, "req", 0, 0, tiled=True).reshape(reqs * block.shape[0], -1)


def core_pair(own, other, core, axis):
    return jnp.where(
        core == 0,
        jnp.concatenate([own, other], axis=axis),
        jnp.concatenate([other, own], axis=axis),
    )


def local(
    tokens,
    cache_entries,
    cache_tenants,
    cached_length,
    tenant_bounds,
    qkv_weight,
    qkv_bias,
    out_weight,
    in_weight,
    in_bias,
    down_weight,
    out_biases,
    norm_gains,
    norm_biases,
):
    nx, ny, nc = lax.axis_size("bx"), lax.axis_size("by"), lax.axis_size("bc")
    core = lax.axis_index("bc")
    chip = lax.axis_index("bx") * ny + lax.axis_index("by")
    block_index = chip * nc + core
    group_size = nx * ny * nc
    groups = group_size // HEADS
    low_bits = groups.bit_length() - 1
    group_index = block_index % groups

    rows, _, column_width = qkv_weight.shape
    qkv_flat = qkv_weight.reshape(rows, 3 * column_width)
    hidden_width = in_weight.shape[1]
    packed = jnp.concatenate([out_weight, in_weight, down_weight], axis=1)
    reqs = lax.axis_size("req")
    qkv_blocks = lax.all_to_all(
        jnp.broadcast_to(qkv_flat[None], (reqs,) + qkv_flat.shape), "req", 0, 0, tiled=True
    ).reshape(reqs, rows, 3, column_width)
    late = gather_rows(packed)
    front = late[:, : column_width + hidden_width]
    sibling = lax.ppermute(front, "bc", swap("bc", nc))
    chip_out = core_pair(front[:, :column_width], sibling[:, :column_width], core, 1)
    chip_in = core_pair(front[:, column_width:], sibling[:, column_width:], core, 1)
    chip_in_bias = lax.dynamic_slice_in_dim(in_bias, chip * nc * hidden_width, nc * hidden_width)
    d_model = late.shape[0]
    quarter_width = d_model // nx
    own_down = late[:, column_width + hidden_width :].reshape(nx, quarter_width, hidden_width)
    row = lax.axis_index("bx")
    received = [lax.dynamic_index_in_dim(own_down, row, 0, keepdims=False)]
    for k in range(1, nx):
        received.append(
            lax.ppermute(
                lax.dynamic_index_in_dim(own_down, row ^ k, 0, keepdims=False),
                "bx",
                [(i, i ^ k) for i in range(nx)],
            )
        )
    from_row = jnp.take(jnp.stack(received), row ^ jnp.arange(nx), axis=0)
    from_sibling = lax.ppermute(from_row, "bc", swap("bc", nc))
    group_down = core_pair(from_row[:, None], from_sibling[:, None], core, 1)

    query_total = tokens.shape[1]
    token_rows = tokens[0]
    qkv_columns = (
        jnp.einsum(
            "tsd,sdce->cet",
            token_rows.reshape(query_total, reqs, rows),
            qkv_blocks,
            preferred_element_type=jnp.float32,
        )
        + qkv_bias[:, :, None]
    ).astype(jnp.bfloat16)
    appended = qkv_columns[1:].transpose(2, 0, 1)[None]

    def from_partner(value, bit_level):
        if bit_level == 0:
            return lax.ppermute(value, "bc", swap("bc", nc))
        return lax.ppermute(value, "by", [(i, i ^ (1 << (bit_level - 1))) for i in range(ny)])

    head_qkv = qkv_columns
    for bit_level in range(low_bits):
        partner = from_partner(head_qkv, bit_level)
        upper_bit = group_index >> bit_level & 1
        head_qkv = jnp.where(
            upper_bit == 1,
            jnp.concatenate([partner, head_qkv], axis=1),
            jnp.concatenate([head_qkv, partner], axis=1),
        )
    queries = head_qkv[0].T
    fresh_count = query_total // groups
    fresh_start = group_index * fresh_count
    fresh_keys = lax.dynamic_slice_in_dim(head_qkv[1], fresh_start, fresh_count, 1).T
    fresh_values = lax.dynamic_slice_in_dim(head_qkv[2], fresh_start, fresh_count, 1).T
    cache_count = cache_entries.shape[2]
    cache_keys = cache_entries[0, 0, :, 0]
    cache_values = cache_entries[0, 0, :, 1]
    cache_position = group_index * cache_count + jnp.arange(cache_count, dtype=jnp.int32)
    tenant_slice = lax.dynamic_slice_in_dim(
        cache_tenants[0], group_index * cache_count, cache_count, 0
    )
    readable = (
        (cache_position < cached_length[0])
        & (tenant_slice >= tenant_bounds[0, 0])
        & (tenant_slice < tenant_bounds[0, 1])
    )
    query_position = jnp.arange(query_total, dtype=jnp.int32)
    fresh_position = fresh_start + jnp.arange(fresh_count, dtype=jnp.int32)
    fresh_visible = fresh_position[None, :] <= query_position[:, None]
    cache_visible = jnp.broadcast_to(readable[None, :], (query_total, cache_count))
    numerator, row_max, row_total = partial_block(
        queries,
        jnp.concatenate([cache_keys, fresh_keys], axis=0),
        jnp.concatenate([cache_values, fresh_values], axis=0),
        jnp.concatenate([cache_visible, fresh_visible], axis=1),
    )
    for bit_level in reversed(range(low_bits)):
        halves = numerator.reshape(2, -1, query_total)
        upper_bit = group_index >> bit_level & 1
        kept_half = jnp.where(upper_bit == 1, halves[1], halves[0])
        sent_half = jnp.where(upper_bit == 1, halves[0], halves[1])
        sent = jnp.concatenate([sent_half, row_max[None], row_total[None]], axis=0)
        got_back = from_partner(sent, bit_level)
        other_sum, other_max, other_total = got_back[:-2], got_back[-2], got_back[-1]
        joined = jnp.maximum(row_max, other_max)
        scale_kept = jnp.exp(row_max - joined)
        scale_other = jnp.exp(other_max - joined)
        numerator = kept_half * scale_kept[None] + other_sum * scale_other[None]
        row_max, row_total = joined, row_total * scale_kept + other_total * scale_other
    context_columns = (numerator / row_total[None]).astype(jnp.bfloat16)

    block_rows = query_total // (group_size)
    chips = nx * ny
    core_rows = chips * block_rows
    halves = (
        context_columns.reshape(column_width, chips, nc, block_rows)
        .transpose(2, 0, 1, 3)
        .reshape(nc, column_width, core_rows)
    )
    mine = lax.dynamic_index_in_dim(halves, core, 0, keepdims=False)
    theirs = lax.dynamic_index_in_dim(halves, 1 - core, 0, keepdims=False)
    got = lax.ppermute(theirs, "bc", swap("bc", nc))
    chip_columns = core_pair(mine, got, core, 0)
    outgoing = jnp.broadcast_to(chip_columns[None], (chips,) + chip_columns.shape)
    core_context = lax.all_to_all(outgoing, PLANE, 0, 0, tiled=True).reshape(
        group_size * column_width, core_rows
    )
    chip_width = nc * column_width
    column_bias = lax.dynamic_slice_in_dim(out_biases[0], chip * chip_width, chip_width)
    projected_part = (
        jnp.einsum("ct,cd->dt", core_context, chip_out, preferred_element_type=jnp.float32)
        + column_bias[:, None]
    ).astype(jnp.bfloat16)
    spread = jnp.broadcast_to(projected_part[None], (chips,) + projected_part.shape)
    spread, group_down = lax.optimization_barrier((spread, group_down))
    projected = lax.all_to_all(spread, PLANE, 0, 0, tiled=True).reshape(chips * chip_width, core_rows)
    core_tokens = lax.dynamic_index_in_dim(
        token_rows.reshape(chips, nc, block_rows, -1), core, axis=1, keepdims=False
    ).reshape(core_rows, -1)
    residual = core_tokens.T.astype(jnp.float32) + projected.astype(jnp.float32)
    centered = residual - jnp.mean(residual, axis=0, keepdims=True)
    variance = jnp.mean(centered * centered, axis=0, keepdims=True)
    normed_t = (
        centered * lax.rsqrt(variance + 1e-06) * norm_gains[0][:, None] + norm_biases[0][:, None]
    ).astype(jnp.bfloat16)
    inner = jax.nn.gelu(
        jnp.einsum("dt,df->tf", normed_t, chip_in, preferred_element_type=jnp.float32) + chip_in_bias,
        approximate=True,
    ).astype(jnp.bfloat16)
    group_inner = lax.all_to_all(
        jnp.broadcast_to(inner[None], (nx,) + inner.shape), "bx", 0, 0, tiled=True
    ).reshape(nx, core_rows, nc, hidden_width)
    mixed_parts = jnp.einsum(
        "xtcf,xcdf->td", group_inner, group_down, preferred_element_type=jnp.float32
    )
    from_chips = lax.all_to_all(
        mixed_parts.reshape(chips, block_rows, quarter_width), PLANE, 0, 0, tiled=True
    ).reshape(nx, ny, block_rows, quarter_width)
    mixed_rows = from_chips.sum(axis=1).transpose(1, 0, 2).reshape(block_rows, d_model)
    own_normed = lax.dynamic_slice_in_dim(normed_t, chip * block_rows, block_rows, 1).T
    layer_output = layer_norm(
        own_normed.astype(jnp.float32) + mixed_rows + out_biases[1], norm_gains[1], norm_biases[1]
    ).astype(jnp.bfloat16)
    return (layer_output[None], appended)


def solution(mesh):
    req, blk = mesh.devices.shape
    fine = Mesh(mesh.devices.reshape(req, 4, blk // 8, 2), ("req",) + BLK)
    return jax.shard_map(
        local,
        mesh=fine,
        in_specs=(
            P("req", None, None),
            P("req", BLK, None, None, None),
            P("req", None),
            P("req"),
            P("req", None),
            P("req", None, BLK),
            P(None, BLK),
            P("req", BLK),
            P("req", BLK),
            P(),
            P("req", BLK),
            P(),
            P(),
            P(),
        ),
        out_specs=(P("req", BLK, None), P("req", None, None, BLK)),
        check_vma=False,
    )
```

```python
import math

import jax
import jax.numpy as jnp
from jax import lax
from jax.sharding import Mesh
from jax.sharding import PartitionSpec as P

HEADS = 16
HEAD_DIM = 128


MASKED = -1e30
PLANE = ("bx", "by")
BLK = ("bx", "by", "bc")


def swap(axis, n):
    return [(i, i ^ 1) for i in range(n)]


def layer_norm(values, gain_row, shift_row):
    centered = values - jnp.mean(values, axis=-1, keepdims=True)
    variance = jnp.mean(centered * centered, axis=-1, keepdims=True)
    return centered * lax.rsqrt(variance + 1e-06) * gain_row + shift_row


def partial_block(queries, key_rows, value_rows, visible):
    scores = jnp.einsum("qd,kd->qk", queries, key_rows, preferred_element_type=jnp.float32) * (
        1.0 / math.sqrt(HEAD_DIM)
    )
    scores = jnp.where(visible, scores, MASKED)
    row_max = jnp.max(scores, axis=1)
    weights = jnp.where(visible, jnp.exp(scores - row_max[:, None]), 0.0)
    row_total = jnp.sum(weights, axis=1)
    numerator = jnp.einsum(
        "qk,kd->dq", weights.astype(jnp.bfloat16), value_rows, preferred_element_type=jnp.float32
    )
    return (numerator, row_max, row_total)


def merge_blocks(earlier_part, later_part):
    joined = jnp.maximum(earlier_part[1], later_part[1])
    scale_earlier = jnp.exp(earlier_part[1] - joined)
    scale_later = jnp.exp(later_part[1] - joined)
    numerator = earlier_part[0] * scale_earlier[:, None] + later_part[0] * scale_later[:, None]
    return (numerator, joined, earlier_part[2] * scale_earlier + later_part[2] * scale_later)


def gather_rows(block):
    reqs = lax.axis_size("req")
    spread = jnp.broadcast_to(block[None], (reqs,) + block.shape)
    return lax.all_to_all(spread, "req", 0, 0, tiled=True).reshape(reqs * block.shape[0], -1)


def core_pair(own, other, core, axis):
    return jnp.where(
        core == 0,
        jnp.concatenate([own, other], axis=axis),
        jnp.concatenate([other, own], axis=axis),
    )


def local(
    tokens,
    cache_entries,
    cache_tenants,
    cached_length,
    tenant_bounds,
    qkv_weight,
    qkv_bias,
    out_weight,
    in_weight,
    in_bias,
    down_weight,
    out_biases,
    norm_gains,
    norm_biases,
):
    nx, ny, nc = lax.axis_size("bx"), lax.axis_size("by"), lax.axis_size("bc")
    core = lax.axis_index("bc")
    chip = lax.axis_index("bx") * ny + lax.axis_index("by")
    block_index = chip * nc + core
    group_size = nx * ny * nc
    groups = group_size // HEADS
    low_bits = groups.bit_length() - 1
    group_index = block_index % groups

    rows, _, column_width = qkv_weight.shape
    qkv_flat = qkv_weight.reshape(rows, 3 * column_width)
    hidden_width = in_weight.shape[1]
    packed = jnp.concatenate([out_weight, in_weight, down_weight], axis=1)
    reqs = lax.axis_size("req")
    qkv_blocks = lax.all_to_all(
        jnp.broadcast_to(qkv_flat[None], (reqs,) + qkv_flat.shape), "req", 0, 0, tiled=True
    ).reshape(reqs, rows, 3, column_width)
    late = gather_rows(packed)
    front = late[:, : column_width + hidden_width]
    sibling = lax.ppermute(front, "bc", swap("bc", nc))
    chip_out = core_pair(front[:, :column_width], sibling[:, :column_width], core, 1)
    chip_in = core_pair(front[:, column_width:], sibling[:, column_width:], core, 1)
    chip_in_bias = lax.dynamic_slice_in_dim(in_bias, chip * nc * hidden_width, nc * hidden_width)
    d_model = late.shape[0]
    quarter_width = d_model // nx
    own_down = late[:, column_width + hidden_width :].reshape(nx, quarter_width, hidden_width)
    row = lax.axis_index("bx")
    received = [lax.dynamic_index_in_dim(own_down, row, 0, keepdims=False)]
    for k in range(1, nx):
        received.append(
            lax.ppermute(
                lax.dynamic_index_in_dim(own_down, row ^ k, 0, keepdims=False),
                "bx",
                [(i, i ^ k) for i in range(nx)],
            )
        )
    from_row = jnp.take(jnp.stack(received), row ^ jnp.arange(nx), axis=0)
    from_sibling = lax.ppermute(from_row, "bc", swap("bc", nc))
    group_down = core_pair(from_row[:, None], from_sibling[:, None], core, 1)

    query_total = tokens.shape[1]
    token_rows = tokens[0]
    qkv_columns = (
        jnp.einsum(
            "tsd,sdce->cet",
            token_rows.reshape(query_total, reqs, rows),
            qkv_blocks,
            preferred_element_type=jnp.float32,
        )
        + qkv_bias[:, :, None]
    ).astype(jnp.bfloat16)
    appended = qkv_columns[1:].transpose(2, 0, 1)[None]

    def from_partner(value, bit_level):
        if bit_level == 0:
            return lax.ppermute(value, "bc", swap("bc", nc))
        return lax.ppermute(value, "by", [(i, i ^ (1 << (bit_level - 1))) for i in range(ny)])

    upper = group_index >> 1 & 1
    partner = from_partner(qkv_columns, 1)
    head_qkv = jnp.where(
        upper == 1,
        jnp.stack([partner, qkv_columns], axis=1),
        jnp.stack([qkv_columns, partner], axis=1),
    )
    partner = from_partner(head_qkv, 0)
    head_qkv = jnp.where(
        core == 1, jnp.stack([partner, head_qkv], axis=2), jnp.stack([head_qkv, partner], axis=2)
    ).reshape(3, groups * column_width, query_total)
    queries = head_qkv[0].T
    fresh_count = query_total // groups
    fresh_start = group_index * fresh_count
    fresh_keys = lax.dynamic_slice_in_dim(head_qkv[1], fresh_start, fresh_count, 1).T
    fresh_values = lax.dynamic_slice_in_dim(head_qkv[2], fresh_start, fresh_count, 1).T
    cache_count = cache_entries.shape[2]
    cache_keys = cache_entries[0, 0, :, 0]
    cache_values = cache_entries[0, 0, :, 1]
    cache_position = group_index * cache_count + jnp.arange(cache_count, dtype=jnp.int32)
    tenant_slice = lax.dynamic_slice_in_dim(
        cache_tenants[0], group_index * cache_count, cache_count, 0
    )
    readable = (
        (cache_position < cached_length[0])
        & (tenant_slice >= tenant_bounds[0, 0])
        & (tenant_slice < tenant_bounds[0, 1])
    )
    query_position = jnp.arange(query_total, dtype=jnp.int32)
    fresh_position = fresh_start + jnp.arange(fresh_count, dtype=jnp.int32)
    fresh_visible = fresh_position[None, :] <= query_position[:, None]
    cache_visible = jnp.broadcast_to(readable[None, :], (query_total, cache_count))
    numerator, row_max, row_total = partial_block(
        queries,
        jnp.concatenate([cache_keys, fresh_keys], axis=0),
        jnp.concatenate([cache_values, fresh_values], axis=0),
        jnp.concatenate([cache_visible, fresh_visible], axis=1),
    )
    def merge_level(kept_half, sent_half, bit_level):
        sent = jnp.concatenate([sent_half, row_max[None], row_total[None]], axis=0)
        got_back = from_partner(sent, bit_level)
        other_sum, other_max, other_total = got_back[:-2], got_back[-2], got_back[-1]
        joined = jnp.maximum(row_max, other_max)
        scale_kept = jnp.exp(row_max - joined)
        scale_other = jnp.exp(other_max - joined)
        merged = kept_half * scale_kept[None] + other_sum * scale_other[None]
        return merged, joined, row_total * scale_kept + other_total * scale_other

    by_bits = numerator.reshape(2, 2, column_width, query_total)
    kept_half = jnp.where(core == 1, by_bits[:, 1], by_bits[:, 0]).reshape(2 * column_width, query_total)
    sent_half = jnp.where(core == 1, by_bits[:, 0], by_bits[:, 1]).reshape(2 * column_width, query_total)
    numerator, row_max, row_total = merge_level(kept_half, sent_half, 0)
    by_bits = numerator.reshape(2, column_width, query_total)
    kept_half = jnp.where(upper == 1, by_bits[1], by_bits[0])
    sent_half = jnp.where(upper == 1, by_bits[0], by_bits[1])
    numerator, row_max, row_total = merge_level(kept_half, sent_half, 1)
    context_columns = (numerator / row_total[None]).astype(jnp.bfloat16)

    block_rows = query_total // (group_size)
    chips = nx * ny
    core_rows = chips * block_rows
    halves = (
        context_columns.reshape(column_width, chips, nc, block_rows)
        .transpose(2, 0, 1, 3)
        .reshape(nc, column_width, core_rows)
    )
    mine = lax.dynamic_index_in_dim(halves, core, 0, keepdims=False)
    theirs = lax.dynamic_index_in_dim(halves, 1 - core, 0, keepdims=False)
    got = lax.ppermute(theirs, "bc", swap("bc", nc))
    chip_columns = core_pair(mine, got, core, 0)
    outgoing = jnp.broadcast_to(chip_columns[None], (chips,) + chip_columns.shape)
    core_context = lax.all_to_all(outgoing, PLANE, 0, 0, tiled=True).reshape(
        group_size * column_width, core_rows
    )
    chip_width = nc * column_width
    column_bias = lax.dynamic_slice_in_dim(out_biases[0], chip * chip_width, chip_width)
    projected_part = (
        jnp.einsum("ct,cd->dt", core_context, chip_out, preferred_element_type=jnp.float32)
        + column_bias[:, None]
    ).astype(jnp.bfloat16)
    spread = jnp.broadcast_to(projected_part[None], (chips,) + projected_part.shape)
    spread, group_down = lax.optimization_barrier((spread, group_down))
    projected = lax.all_to_all(spread, PLANE, 0, 0, tiled=True).reshape(chips * chip_width, core_rows)
    core_tokens = lax.dynamic_index_in_dim(
        token_rows.reshape(chips, nc, block_rows, -1), core, axis=1, keepdims=False
    ).reshape(core_rows, -1)
    residual = core_tokens.T.astype(jnp.float32) + projected.astype(jnp.float32)
    centered = residual - jnp.mean(residual, axis=0, keepdims=True)
    variance = jnp.mean(centered * centered, axis=0, keepdims=True)
    normed_t = (
        centered * lax.rsqrt(variance + 1e-06) * norm_gains[0][:, None] + norm_biases[0][:, None]
    ).astype(jnp.bfloat16)
    inner = jax.nn.gelu(
        jnp.einsum("dt,df->tf", normed_t, chip_in, preferred_element_type=jnp.float32) + chip_in_bias,
        approximate=True,
    ).astype(jnp.bfloat16)
    group_inner = lax.all_to_all(
        jnp.broadcast_to(inner[None], (nx,) + inner.shape), "bx", 0, 0, tiled=True
    ).reshape(nx, core_rows, nc, hidden_width)
    mixed_parts = jnp.einsum(
        "xtcf,xcdf->td", group_inner, group_down, preferred_element_type=jnp.float32
    )
    from_chips = lax.all_to_all(
        mixed_parts.reshape(chips, block_rows, quarter_width), PLANE, 0, 0, tiled=True
    ).reshape(nx, ny, block_rows, quarter_width)
    mixed_rows = from_chips.sum(axis=1).transpose(1, 0, 2).reshape(block_rows, d_model)
    own_normed = lax.dynamic_slice_in_dim(normed_t, chip * block_rows, block_rows, 1).T
    layer_output = layer_norm(
        own_normed.astype(jnp.float32) + mixed_rows + out_biases[1], norm_gains[1], norm_biases[1]
    ).astype(jnp.bfloat16)
    return (layer_output[None], appended)


def solution(mesh):
    req, blk = mesh.devices.shape
    fine = Mesh(mesh.devices.reshape(req, 4, blk // 8, 2), ("req",) + BLK)
    return jax.shard_map(
        local,
        mesh=fine,
        in_specs=(
            P("req", None, None),
            P("req", BLK, None, None, None),
            P("req", None),
            P("req"),
            P("req", None),
            P("req", None, BLK),
            P(None, BLK),
            P("req", BLK),
            P("req", BLK),
            P(),
            P("req", BLK),
            P(),
            P(),
            P(),
        ),
        out_specs=(P("req", BLK, None), P("req", None, None, BLK)),
        check_vma=False,
    )
```

```python
import math

import jax
import jax.numpy as jnp
from jax import lax
from jax.sharding import Mesh
from jax.sharding import PartitionSpec as P

HEADS = 16
HEAD_DIM = 128


MASKED = -1e30
PLANE = ("bx", "by")
BLK = ("bx", "by", "bc")


def swap(axis, n):
    return [(i, i ^ 1) for i in range(n)]


def layer_norm(values, gain_row, shift_row):
    centered = values - jnp.mean(values, axis=-1, keepdims=True)
    variance = jnp.mean(centered * centered, axis=-1, keepdims=True)
    return centered * lax.rsqrt(variance + 1e-06) * gain_row + shift_row


def partial_block(queries, key_rows, value_rows, visible):
    scores = jnp.einsum("qd,kd->qk", queries, key_rows, preferred_element_type=jnp.float32) * (
        1.0 / math.sqrt(HEAD_DIM)
    )
    scores = jnp.where(visible, scores, MASKED)
    row_max = jnp.max(scores, axis=1)
    weights = jnp.where(visible, jnp.exp(scores - row_max[:, None]), 0.0)
    row_total = jnp.sum(weights, axis=1)
    numerator = jnp.einsum(
        "qk,kd->dq", weights.astype(jnp.bfloat16), value_rows, preferred_element_type=jnp.float32
    )
    return (numerator, row_max, row_total)


def merge_blocks(earlier_part, later_part):
    joined = jnp.maximum(earlier_part[1], later_part[1])
    scale_earlier = jnp.exp(earlier_part[1] - joined)
    scale_later = jnp.exp(later_part[1] - joined)
    numerator = earlier_part[0] * scale_earlier[:, None] + later_part[0] * scale_later[:, None]
    return (numerator, joined, earlier_part[2] * scale_earlier + later_part[2] * scale_later)


def gather_rows(block):
    reqs = lax.axis_size("req")
    spread = jnp.broadcast_to(block[None], (reqs,) + block.shape)
    return lax.all_to_all(spread, "req", 0, 0, tiled=True).reshape(reqs * block.shape[0], -1)


def core_pair(own, other, core, axis):
    return jnp.where(
        core == 0,
        jnp.concatenate([own, other], axis=axis),
        jnp.concatenate([other, own], axis=axis),
    )


def local(
    tokens,
    cache_entries,
    cache_tenants,
    cached_length,
    tenant_bounds,
    qkv_weight,
    qkv_bias,
    out_weight,
    in_weight,
    in_bias,
    down_weight,
    out_biases,
    norm_gains,
    norm_biases,
):
    nx, ny, nc = lax.axis_size("bx"), lax.axis_size("by"), lax.axis_size("bc")
    core = lax.axis_index("bc")
    chip = lax.axis_index("bx") * ny + lax.axis_index("by")
    block_index = chip * nc + core
    group_size = nx * ny * nc
    groups = group_size // HEADS
    low_bits = groups.bit_length() - 1
    group_index = block_index % groups

    rows, _, column_width = qkv_weight.shape
    qkv_flat = qkv_weight.reshape(rows, 3 * column_width)
    hidden_width = in_weight.shape[1]
    packed = jnp.concatenate([out_weight, in_weight, down_weight], axis=1)
    reqs = lax.axis_size("req")
    qkv_blocks = lax.all_to_all(
        jnp.broadcast_to(qkv_flat[None], (reqs,) + qkv_flat.shape), "req", 0, 0, tiled=True
    ).reshape(reqs, rows, 3, column_width)
    late = gather_rows(packed)
    front = late[:, : column_width + hidden_width]
    sibling = lax.ppermute(front, "bc", swap("bc", nc))
    chip_out = core_pair(front[:, :column_width], sibling[:, :column_width], core, 1)
    chip_in = core_pair(front[:, column_width:], sibling[:, column_width:], core, 1)
    chip_in_bias = lax.dynamic_slice_in_dim(in_bias, chip * nc * hidden_width, nc * hidden_width)
    d_model = late.shape[0]
    quarter_width = d_model // nx
    own_down = late[:, column_width + hidden_width :].reshape(nx, quarter_width, hidden_width)
    query_total = tokens.shape[1]
    token_rows = tokens[0]
    qkv_columns = (
        jnp.einsum(
            "tsd,sdce->cet",
            token_rows.reshape(query_total, reqs, rows),
            qkv_blocks,
            preferred_element_type=jnp.float32,
        )
        + qkv_bias[:, :, None]
    ).astype(jnp.bfloat16)
    appended = qkv_columns[1:].transpose(2, 0, 1)[None]

    def from_partner(value, bit_level):
        if bit_level == 0:
            return lax.ppermute(value, "bc", swap("bc", nc))
        return lax.ppermute(value, "by", [(i, i ^ (1 << (bit_level - 1))) for i in range(ny)])

    upper = group_index >> 1 & 1
    partner = from_partner(qkv_columns, 1)
    head_qkv = jnp.where(
        upper == 1,
        jnp.stack([partner, qkv_columns], axis=1),
        jnp.stack([qkv_columns, partner], axis=1),
    )
    partner = from_partner(head_qkv, 0)
    head_qkv = jnp.where(
        core == 1, jnp.stack([partner, head_qkv], axis=2), jnp.stack([head_qkv, partner], axis=2)
    ).reshape(3, groups * column_width, query_total)
    queries = head_qkv[0].T
    fresh_count = query_total // groups
    fresh_start = group_index * fresh_count
    fresh_keys = lax.dynamic_slice_in_dim(head_qkv[1], fresh_start, fresh_count, 1).T
    fresh_values = lax.dynamic_slice_in_dim(head_qkv[2], fresh_start, fresh_count, 1).T
    cache_count = cache_entries.shape[2]
    cache_keys = cache_entries[0, 0, :, 0]
    cache_values = cache_entries[0, 0, :, 1]
    cache_position = group_index * cache_count + jnp.arange(cache_count, dtype=jnp.int32)
    tenant_slice = lax.dynamic_slice_in_dim(
        cache_tenants[0], group_index * cache_count, cache_count, 0
    )
    readable = (
        (cache_position < cached_length[0])
        & (tenant_slice >= tenant_bounds[0, 0])
        & (tenant_slice < tenant_bounds[0, 1])
    )
    query_position = jnp.arange(query_total, dtype=jnp.int32)
    fresh_position = fresh_start + jnp.arange(fresh_count, dtype=jnp.int32)
    fresh_visible = fresh_position[None, :] <= query_position[:, None]
    cache_visible = jnp.broadcast_to(readable[None, :], (query_total, cache_count))
    numerator, row_max, row_total = partial_block(
        queries,
        jnp.concatenate([cache_keys, fresh_keys], axis=0),
        jnp.concatenate([cache_values, fresh_values], axis=0),
        jnp.concatenate([cache_visible, fresh_visible], axis=1),
    )
    def merge_level(kept_half, sent_half, bit_level):
        sent = jnp.concatenate([sent_half, row_max[None], row_total[None]], axis=0)
        got_back = from_partner(sent, bit_level)
        other_sum, other_max, other_total = got_back[:-2], got_back[-2], got_back[-1]
        joined = jnp.maximum(row_max, other_max)
        scale_kept = jnp.exp(row_max - joined)
        scale_other = jnp.exp(other_max - joined)
        merged = kept_half * scale_kept[None] + other_sum * scale_other[None]
        return merged, joined, row_total * scale_kept + other_total * scale_other

    by_bits = numerator.reshape(2, 2, column_width, query_total)
    kept_half = jnp.where(core == 1, by_bits[:, 1], by_bits[:, 0]).reshape(2 * column_width, query_total)
    sent_half = jnp.where(core == 1, by_bits[:, 0], by_bits[:, 1]).reshape(2 * column_width, query_total)
    numerator, row_max, row_total = merge_level(kept_half, sent_half, 0)
    by_bits = numerator.reshape(2, column_width, query_total)
    kept_half = jnp.where(upper == 1, by_bits[1], by_bits[0])
    sent_half = jnp.where(upper == 1, by_bits[0], by_bits[1])
    numerator, row_max, row_total = merge_level(kept_half, sent_half, 1)
    context_columns = (numerator / row_total[None]).astype(jnp.bfloat16)

    block_rows = query_total // (group_size)
    chips = nx * ny
    core_rows = chips * block_rows
    halves = (
        context_columns.reshape(column_width, chips, nc, block_rows)
        .transpose(2, 0, 1, 3)
        .reshape(nc, column_width, core_rows)
    )
    mine = lax.dynamic_index_in_dim(halves, core, 0, keepdims=False)
    theirs = lax.dynamic_index_in_dim(halves, 1 - core, 0, keepdims=False)
    got = lax.ppermute(theirs, "bc", swap("bc", nc))
    chip_columns = core_pair(mine, got, core, 0)
    outgoing = jnp.broadcast_to(chip_columns[None], (chips,) + chip_columns.shape)
    core_context = lax.all_to_all(outgoing, PLANE, 0, 0, tiled=True).reshape(
        group_size * column_width, core_rows
    )
    chip_width = nc * column_width
    column_bias = lax.dynamic_slice_in_dim(out_biases[0], chip * chip_width, chip_width)
    projected_part = (
        jnp.einsum("ct,cd->dt", core_context, chip_out, preferred_element_type=jnp.float32)
        + column_bias[:, None]
    ).astype(jnp.bfloat16)
    spread = jnp.broadcast_to(projected_part[None], (chips,) + projected_part.shape)
    spread, own_down = lax.optimization_barrier((spread, own_down))
    row = lax.axis_index("bx")
    received = [lax.dynamic_index_in_dim(own_down, row, 0, keepdims=False)]
    for k in range(1, nx):
        received.append(
            lax.ppermute(
                lax.dynamic_index_in_dim(own_down, row ^ k, 0, keepdims=False),
                "bx",
                [(i, i ^ k) for i in range(nx)],
            )
        )
    from_row = jnp.take(jnp.stack(received), row ^ jnp.arange(nx), axis=0)
    from_sibling = lax.ppermute(from_row, "bc", swap("bc", nc))
    group_down = core_pair(from_row[:, None], from_sibling[:, None], core, 1)
    projected = lax.all_to_all(spread, PLANE, 0, 0, tiled=True).reshape(chips * chip_width, core_rows)
    core_tokens = lax.dynamic_index_in_dim(
        token_rows.reshape(chips, nc, block_rows, -1), core, axis=1, keepdims=False
    ).reshape(core_rows, -1)
    residual = core_tokens.T.astype(jnp.float32) + projected.astype(jnp.float32)
    centered = residual - jnp.mean(residual, axis=0, keepdims=True)
    variance = jnp.mean(centered * centered, axis=0, keepdims=True)
    normed_t = (
        centered * lax.rsqrt(variance + 1e-06) * norm_gains[0][:, None] + norm_biases[0][:, None]
    ).astype(jnp.bfloat16)
    inner = jax.nn.gelu(
        jnp.einsum("dt,df->tf", normed_t, chip_in, preferred_element_type=jnp.float32) + chip_in_bias,
        approximate=True,
    ).astype(jnp.bfloat16)
    group_inner = lax.all_to_all(
        jnp.broadcast_to(inner[None], (nx,) + inner.shape), "bx", 0, 0, tiled=True
    ).reshape(nx, core_rows, nc, hidden_width)
    mixed_parts = jnp.einsum(
        "xtcf,xcdf->td", group_inner, group_down, preferred_element_type=jnp.float32
    )
    from_chips = lax.all_to_all(
        mixed_parts.reshape(chips, block_rows, quarter_width), PLANE, 0, 0, tiled=True
    ).reshape(nx, ny, block_rows, quarter_width)
    mixed_rows = from_chips.sum(axis=1).transpose(1, 0, 2).reshape(block_rows, d_model)
    own_normed = lax.dynamic_slice_in_dim(normed_t, chip * block_rows, block_rows, 1).T
    layer_output = layer_norm(
        own_normed.astype(jnp.float32) + mixed_rows + out_biases[1], norm_gains[1], norm_biases[1]
    ).astype(jnp.bfloat16)
    return (layer_output[None], appended)


def solution(mesh):
    req, blk = mesh.devices.shape
    fine = Mesh(mesh.devices.reshape(req, 4, blk // 8, 2), ("req",) + BLK)
    return jax.shard_map(
        local,
        mesh=fine,
        in_specs=(
            P("req", None, None),
            P("req", BLK, None, None, None),
            P("req", None),
            P("req"),
            P("req", None),
            P("req", None, BLK),
            P(None, BLK),
            P("req", BLK),
            P("req", BLK),
            P(),
            P("req", BLK),
            P(),
            P(),
            P(),
        ),
        out_specs=(P("req", BLK, None), P("req", None, None, BLK)),
        check_vma=False,
    )
```

```python
import math

import jax
import jax.numpy as jnp
from jax import lax
from jax.sharding import Mesh
from jax.sharding import PartitionSpec as P

HEADS = 16
HEAD_DIM = 128


MASKED = -1e30
PLANE = ("bx", "by")
BLK = ("bx", "by", "bc")


def swap(axis, n):
    return [(i, i ^ 1) for i in range(n)]


def layer_norm(values, gain_row, shift_row):
    centered = values - jnp.mean(values, axis=-1, keepdims=True)
    variance = jnp.mean(centered * centered, axis=-1, keepdims=True)
    return centered * lax.rsqrt(variance + 1e-06) * gain_row + shift_row


def partial_block(queries, key_rows, value_rows, visible):
    scores = jnp.einsum("qd,kd->qk", queries, key_rows, preferred_element_type=jnp.float32) * (
        1.0 / math.sqrt(HEAD_DIM)
    )
    scores = jnp.where(visible, scores, MASKED)
    row_max = jnp.max(scores, axis=1)
    weights = jnp.where(visible, jnp.exp(scores - row_max[:, None]), 0.0)
    row_total = jnp.sum(weights, axis=1)
    numerator = jnp.einsum(
        "qk,kd->dq", weights.astype(jnp.bfloat16), value_rows, preferred_element_type=jnp.float32
    )
    return (numerator, row_max, row_total)


def merge_blocks(earlier_part, later_part):
    joined = jnp.maximum(earlier_part[1], later_part[1])
    scale_earlier = jnp.exp(earlier_part[1] - joined)
    scale_later = jnp.exp(later_part[1] - joined)
    numerator = earlier_part[0] * scale_earlier[:, None] + later_part[0] * scale_later[:, None]
    return (numerator, joined, earlier_part[2] * scale_earlier + later_part[2] * scale_later)


def gather_rows(block):
    reqs = lax.axis_size("req")
    spread = jnp.broadcast_to(block[None], (reqs,) + block.shape)
    return lax.all_to_all(spread, "req", 0, 0, tiled=True).reshape(reqs * block.shape[0], -1)


def core_pair(own, other, core, axis):
    return jnp.where(
        core == 0,
        jnp.concatenate([own, other], axis=axis),
        jnp.concatenate([other, own], axis=axis),
    )


def local(
    tokens,
    cache_entries,
    cache_tenants,
    cached_length,
    tenant_bounds,
    qkv_weight,
    qkv_bias,
    out_weight,
    in_weight,
    in_bias,
    down_weight,
    out_biases,
    norm_gains,
    norm_biases,
):
    nx, ny, nc = lax.axis_size("bx"), lax.axis_size("by"), lax.axis_size("bc")
    core = lax.axis_index("bc")
    chip = lax.axis_index("bx") * ny + lax.axis_index("by")
    block_index = chip * nc + core
    group_size = nx * ny * nc
    groups = group_size // HEADS
    low_bits = groups.bit_length() - 1
    group_index = block_index % groups

    rows, _, column_width = qkv_weight.shape
    qkv_flat = qkv_weight.reshape(rows, 3 * column_width)
    hidden_width = in_weight.shape[1]
    packed = jnp.concatenate([out_weight, in_weight, down_weight], axis=1)
    reqs = lax.axis_size("req")
    qkv_blocks = lax.all_to_all(
        jnp.broadcast_to(qkv_flat[None], (reqs,) + qkv_flat.shape), "req", 0, 0, tiled=True
    ).reshape(reqs, rows, 3, column_width)
    late = gather_rows(packed)
    front = late[:, : column_width + hidden_width]
    sibling = lax.ppermute(front, "bc", swap("bc", nc))
    chip_out = core_pair(front[:, :column_width], sibling[:, :column_width], core, 1)
    chip_in = core_pair(front[:, column_width:], sibling[:, column_width:], core, 1)
    chip_in_bias = lax.dynamic_slice_in_dim(in_bias, chip * nc * hidden_width, nc * hidden_width)
    d_model = late.shape[0]
    quarter_width = d_model // nx
    own_down = late[:, column_width + hidden_width :].reshape(nx, quarter_width, hidden_width)
    row = lax.axis_index("bx")
    received = [lax.dynamic_index_in_dim(own_down, row, 0, keepdims=False)]
    for k in range(1, nx):
        received.append(
            lax.ppermute(
                lax.dynamic_index_in_dim(own_down, row ^ k, 0, keepdims=False),
                "bx",
                [(i, i ^ k) for i in range(nx)],
            )
        )
    from_row = jnp.take(jnp.stack(received), row ^ jnp.arange(nx), axis=0)
    from_sibling = lax.ppermute(from_row, "bc", swap("bc", nc))
    group_down = core_pair(from_row[:, None], from_sibling[:, None], core, 1)

    query_total = tokens.shape[1]
    token_rows = tokens[0]
    qkv_columns = (
        jnp.einsum(
            "tsd,sdce->cet",
            token_rows.reshape(query_total, reqs, rows),
            qkv_blocks,
            preferred_element_type=jnp.float32,
        )
        + qkv_bias[:, :, None]
    ).astype(jnp.bfloat16)
    appended = qkv_columns[1:].transpose(2, 0, 1)[None]

    def from_partner(value, bit_level):
        if bit_level == 0:
            return lax.ppermute(value, "bc", swap("bc", nc))
        return lax.ppermute(value, "by", [(i, i ^ (1 << (bit_level - 1))) for i in range(ny)])

    upper = group_index >> 1 & 1
    partner = from_partner(qkv_columns, 1)
    head_qkv = jnp.where(
        upper == 1,
        jnp.stack([partner, qkv_columns], axis=1),
        jnp.stack([qkv_columns, partner], axis=1),
    )
    partner = from_partner(head_qkv, 0)
    head_qkv = jnp.where(
        core == 1, jnp.stack([partner, head_qkv], axis=2), jnp.stack([head_qkv, partner], axis=2)
    ).reshape(3, groups * column_width, query_total)
    queries = head_qkv[0].T
    fresh_count = query_total // groups
    fresh_start = group_index * fresh_count
    fresh_keys = lax.dynamic_slice_in_dim(head_qkv[1], fresh_start, fresh_count, 1).T
    fresh_values = lax.dynamic_slice_in_dim(head_qkv[2], fresh_start, fresh_count, 1).T
    cache_count = cache_entries.shape[2]
    cache_keys = cache_entries[0, 0, :, 0]
    cache_values = cache_entries[0, 0, :, 1]
    cache_position = group_index * cache_count + jnp.arange(cache_count, dtype=jnp.int32)
    tenant_slice = lax.dynamic_slice_in_dim(
        cache_tenants[0], group_index * cache_count, cache_count, 0
    )
    readable = (
        (cache_position < cached_length[0])
        & (tenant_slice >= tenant_bounds[0, 0])
        & (tenant_slice < tenant_bounds[0, 1])
    )
    query_position = jnp.arange(query_total, dtype=jnp.int32)
    fresh_position = fresh_start + jnp.arange(fresh_count, dtype=jnp.int32)
    fresh_visible = fresh_position[None, :] <= query_position[:, None]
    cache_visible = jnp.broadcast_to(readable[None, :], (query_total, cache_count))
    numerator, row_max, row_total = partial_block(
        queries,
        jnp.concatenate([cache_keys, fresh_keys], axis=0),
        jnp.concatenate([cache_values, fresh_values], axis=0),
        jnp.concatenate([cache_visible, fresh_visible], axis=1),
    )
    def merge_level(kept_half, sent_half, bit_level):
        sent = jnp.concatenate([sent_half, row_max[None], row_total[None]], axis=0)
        got_back = from_partner(sent, bit_level)
        other_sum, other_max, other_total = got_back[:-2], got_back[-2], got_back[-1]
        joined = jnp.maximum(row_max, other_max)
        scale_kept = jnp.exp(row_max - joined)
        scale_other = jnp.exp(other_max - joined)
        merged = kept_half * scale_kept[None] + other_sum * scale_other[None]
        return merged, joined, row_total * scale_kept + other_total * scale_other

    by_bits = numerator.reshape(2, 2 * column_width, query_total)
    kept_half = jnp.where(upper == 1, by_bits[1], by_bits[0])
    sent_half = jnp.where(upper == 1, by_bits[0], by_bits[1])
    numerator, row_max, row_total = merge_level(kept_half, sent_half, 1)
    numerator, row_max, row_total = merge_level(numerator, numerator, 0)
    context_columns = (numerator / row_total[None]).astype(jnp.bfloat16)

    block_rows = query_total // (group_size)
    chips = nx * ny
    core_rows = chips * block_rows
    chip_columns = lax.dynamic_index_in_dim(
        context_columns.reshape(nc * column_width, chips, nc, block_rows), core, 2, keepdims=False
    ).reshape(nc * column_width, core_rows)
    outgoing = jnp.broadcast_to(chip_columns[None], (chips,) + chip_columns.shape)
    core_context = lax.all_to_all(outgoing, PLANE, 0, 0, tiled=True).reshape(
        group_size * column_width, core_rows
    )
    chip_width = nc * column_width
    column_bias = lax.dynamic_slice_in_dim(out_biases[0], chip * chip_width, chip_width)
    projected_part = (
        jnp.einsum("ct,cd->dt", core_context, chip_out, preferred_element_type=jnp.float32)
        + column_bias[:, None]
    ).astype(jnp.bfloat16)
    spread = jnp.broadcast_to(projected_part[None], (chips,) + projected_part.shape)
    spread, group_down = lax.optimization_barrier((spread, group_down))
    projected = lax.all_to_all(spread, PLANE, 0, 0, tiled=True).reshape(chips * chip_width, core_rows)
    core_tokens = lax.dynamic_index_in_dim(
        token_rows.reshape(chips, nc, block_rows, -1), core, axis=1, keepdims=False
    ).reshape(core_rows, -1)
    residual = core_tokens.T.astype(jnp.float32) + projected.astype(jnp.float32)
    centered = residual - jnp.mean(residual, axis=0, keepdims=True)
    variance = jnp.mean(centered * centered, axis=0, keepdims=True)
    normed_t = (
        centered * lax.rsqrt(variance + 1e-06) * norm_gains[0][:, None] + norm_biases[0][:, None]
    ).astype(jnp.bfloat16)
    inner = jax.nn.gelu(
        jnp.einsum("dt,df->tf", normed_t, chip_in, preferred_element_type=jnp.float32) + chip_in_bias,
        approximate=True,
    ).astype(jnp.bfloat16)
    group_inner = lax.all_to_all(
        jnp.broadcast_to(inner[None], (nx,) + inner.shape), "bx", 0, 0, tiled=True
    ).reshape(nx, core_rows, nc, hidden_width)
    mixed_parts = jnp.einsum(
        "xtcf,xcdf->td", group_inner, group_down, preferred_element_type=jnp.float32
    )
    from_chips = lax.all_to_all(
        mixed_parts.reshape(chips, block_rows, quarter_width), PLANE, 0, 0, tiled=True
    ).reshape(nx, ny, block_rows, quarter_width)
    mixed_rows = from_chips.sum(axis=1).transpose(1, 0, 2).reshape(block_rows, d_model)
    own_normed = lax.dynamic_slice_in_dim(normed_t, chip * block_rows, block_rows, 1).T
    layer_output = layer_norm(
        own_normed.astype(jnp.float32) + mixed_rows + out_biases[1], norm_gains[1], norm_biases[1]
    ).astype(jnp.bfloat16)
    return (layer_output[None], appended)


def solution(mesh):
    req, blk = mesh.devices.shape
    fine = Mesh(mesh.devices.reshape(req, 4, blk // 8, 2), ("req",) + BLK)
    return jax.shard_map(
        local,
        mesh=fine,
        in_specs=(
            P("req", None, None),
            P("req", BLK, None, None, None),
            P("req", None),
            P("req"),
            P("req", None),
            P("req", None, BLK),
            P(None, BLK),
            P("req", BLK),
            P("req", BLK),
            P(),
            P("req", BLK),
            P(),
            P(),
            P(),
        ),
        out_specs=(P("req", BLK, None), P("req", None, None, BLK)),
        check_vma=False,
    )
```

```python
import math

import jax
import jax.numpy as jnp
from jax import lax
from jax.sharding import Mesh
from jax.sharding import PartitionSpec as P

HEADS = 16
HEAD_DIM = 128


MASKED = -1e30
PLANE = ("bx", "by")
BLK = ("bx", "by", "bc")


def swap(axis, n):
    return [(i, i ^ 1) for i in range(n)]


def layer_norm(values, gain_row, shift_row):
    centered = values - jnp.mean(values, axis=-1, keepdims=True)
    variance = jnp.mean(centered * centered, axis=-1, keepdims=True)
    return centered * lax.rsqrt(variance + 1e-06) * gain_row + shift_row


def partial_block(queries, key_rows, value_rows, visible):
    scores = jnp.einsum("qd,kd->qk", queries, key_rows, preferred_element_type=jnp.float32) * (
        1.0 / math.sqrt(HEAD_DIM)
    )
    scores = jnp.where(visible, scores, MASKED)
    row_max = jnp.max(scores, axis=1)
    weights = jnp.where(visible, jnp.exp(scores - row_max[:, None]), 0.0)
    row_total = jnp.sum(weights, axis=1)
    numerator = jnp.einsum(
        "qk,kd->dq", weights.astype(jnp.bfloat16), value_rows, preferred_element_type=jnp.float32
    )
    return (numerator, row_max, row_total)


def merge_blocks(earlier_part, later_part):
    joined = jnp.maximum(earlier_part[1], later_part[1])
    scale_earlier = jnp.exp(earlier_part[1] - joined)
    scale_later = jnp.exp(later_part[1] - joined)
    numerator = earlier_part[0] * scale_earlier[:, None] + later_part[0] * scale_later[:, None]
    return (numerator, joined, earlier_part[2] * scale_earlier + later_part[2] * scale_later)


def gather_rows(block):
    reqs = lax.axis_size("req")
    spread = jnp.broadcast_to(block[None], (reqs,) + block.shape)
    return lax.all_to_all(spread, "req", 0, 0, tiled=True).reshape(reqs * block.shape[0], -1)


def core_pair(own, other, core, axis):
    return jnp.where(
        core == 0,
        jnp.concatenate([own, other], axis=axis),
        jnp.concatenate([other, own], axis=axis),
    )


def local(
    tokens,
    cache_entries,
    cache_tenants,
    cached_length,
    tenant_bounds,
    qkv_weight,
    qkv_bias,
    out_weight,
    in_weight,
    in_bias,
    down_weight,
    out_biases,
    norm_gains,
    norm_biases,
):
    nx, ny, nc = lax.axis_size("bx"), lax.axis_size("by"), lax.axis_size("bc")
    core = lax.axis_index("bc")
    chip = lax.axis_index("bx") * ny + lax.axis_index("by")
    block_index = chip * nc + core
    group_size = nx * ny * nc
    groups = group_size // HEADS
    low_bits = groups.bit_length() - 1
    group_index = block_index % groups

    rows, _, column_width = qkv_weight.shape
    qkv_flat = qkv_weight.reshape(rows, 3 * column_width)
    hidden_width = in_weight.shape[1]
    packed = jnp.concatenate([out_weight, in_weight, down_weight], axis=1)
    reqs = lax.axis_size("req")
    qkv_blocks = lax.all_to_all(
        jnp.broadcast_to(qkv_flat[None], (reqs,) + qkv_flat.shape), "req", 0, 0, tiled=True
    ).reshape(reqs, rows, 3, column_width)
    late = gather_rows(packed)
    front = late[:, : column_width + hidden_width]
    sibling = lax.ppermute(front, "bc", swap("bc", nc))
    chip_out = core_pair(front[:, :column_width], sibling[:, :column_width], core, 1)
    chip_in = core_pair(front[:, column_width:], sibling[:, column_width:], core, 1)
    chip_in_bias = lax.dynamic_slice_in_dim(in_bias, chip * nc * hidden_width, nc * hidden_width)
    d_model = late.shape[0]
    quarter_width = d_model // nx
    own_down = late[:, column_width + hidden_width :].reshape(nx, quarter_width, hidden_width)
    row = lax.axis_index("bx")
    received = [lax.dynamic_index_in_dim(own_down, row, 0, keepdims=False)]
    for k in range(1, nx):
        received.append(
            lax.ppermute(
                lax.dynamic_index_in_dim(own_down, row ^ k, 0, keepdims=False),
                "bx",
                [(i, i ^ k) for i in range(nx)],
            )
        )
    from_row = jnp.take(jnp.stack(received), row ^ jnp.arange(nx), axis=0)
    from_sibling = lax.ppermute(from_row, "bc", swap("bc", nc))
    group_down = core_pair(from_row[:, None], from_sibling[:, None], core, 1)

    query_total = tokens.shape[1]
    token_rows = tokens[0]
    qkv_columns = (
        jnp.einsum(
            "tsd,sdce->cet",
            token_rows.reshape(query_total, reqs, rows),
            qkv_blocks,
            preferred_element_type=jnp.float32,
        )
        + qkv_bias[:, :, None]
    ).astype(jnp.bfloat16)
    appended = qkv_columns[1:].transpose(2, 0, 1)[None]

    def from_partner(value, bit_level):
        if bit_level == 0:
            return lax.ppermute(value, "bc", swap("bc", nc))
        return lax.ppermute(value, "by", [(i, i ^ (1 << (bit_level - 1))) for i in range(ny)])

    upper = group_index >> 1 & 1
    quarter = query_total // groups
    chip_tokens = 2 * quarter

    def packed(q_part, kv_part):
        kv_flat = jnp.swapaxes(kv_part, -3, -2)
        kv_flat = kv_flat.reshape(kv_flat.shape[:-2] + (-1,))
        return jnp.concatenate([q_part, kv_flat], axis=-1)

    own_kv = qkv_columns[1:]
    got = from_partner(
        packed(qkv_columns[0], lax.dynamic_slice_in_dim(own_kv, (1 - upper) * chip_tokens, chip_tokens, 2)), 1
    )
    mine_kv = lax.dynamic_slice_in_dim(own_kv, upper * chip_tokens, chip_tokens, 2)
    got_kv = jnp.swapaxes(got[:, query_total:].reshape(column_width, 2, chip_tokens), 0, 1)
    q2 = jnp.where(
        upper == 1, jnp.stack([got[:, :query_total], qkv_columns[0]]), jnp.stack([qkv_columns[0], got[:, :query_total]])
    )
    kv2 = jnp.where(upper == 1, jnp.stack([got_kv, mine_kv]), jnp.stack([mine_kv, got_kv]))
    got = from_partner(packed(q2, lax.dynamic_slice_in_dim(kv2, (1 - core) * quarter, quarter, 3)), 0)
    sibling_q = got[:, :, :query_total]
    sibling_kv = jnp.swapaxes(got[:, :, query_total:].reshape(2, column_width, 2, quarter), 1, 2)
    mine_kv = lax.dynamic_slice_in_dim(kv2, core * quarter, quarter, 3)
    q4 = jnp.where(core == 1, jnp.stack([sibling_q, q2], 1), jnp.stack([q2, sibling_q], 1))
    kv4 = jnp.where(core == 1, jnp.stack([sibling_kv, mine_kv], 1), jnp.stack([mine_kv, sibling_kv], 1))
    queries = q4.reshape(groups * column_width, query_total).T
    head_kv = kv4.transpose(2, 0, 1, 3, 4).reshape(2, groups * column_width, quarter)
    fresh_count = quarter
    fresh_keys = head_kv[0].T
    fresh_values = head_kv[1].T
    fresh_start = group_index * fresh_count
    cache_count = cache_entries.shape[2]
    cache_keys = cache_entries[0, 0, :, 0]
    cache_values = cache_entries[0, 0, :, 1]
    cache_position = group_index * cache_count + jnp.arange(cache_count, dtype=jnp.int32)
    tenant_slice = lax.dynamic_slice_in_dim(
        cache_tenants[0], group_index * cache_count, cache_count, 0
    )
    readable = (
        (cache_position < cached_length[0])
        & (tenant_slice >= tenant_bounds[0, 0])
        & (tenant_slice < tenant_bounds[0, 1])
    )
    query_position = jnp.arange(query_total, dtype=jnp.int32)
    fresh_position = fresh_start + jnp.arange(fresh_count, dtype=jnp.int32)
    fresh_visible = fresh_position[None, :] <= query_position[:, None]
    cache_visible = jnp.broadcast_to(readable[None, :], (query_total, cache_count))
    numerator, row_max, row_total = partial_block(
        queries,
        jnp.concatenate([cache_keys, fresh_keys], axis=0),
        jnp.concatenate([cache_values, fresh_values], axis=0),
        jnp.concatenate([cache_visible, fresh_visible], axis=1),
    )
    def merge_level(kept_half, sent_half, bit_level):
        sent = jnp.concatenate([sent_half, row_max[None], row_total[None]], axis=0)
        got_back = from_partner(sent, bit_level)
        other_sum, other_max, other_total = got_back[:-2], got_back[-2], got_back[-1]
        joined = jnp.maximum(row_max, other_max)
        scale_kept = jnp.exp(row_max - joined)
        scale_other = jnp.exp(other_max - joined)
        merged = kept_half * scale_kept[None] + other_sum * scale_other[None]
        return merged, joined, row_total * scale_kept + other_total * scale_other

    by_bits = numerator.reshape(2, 2 * column_width, query_total)
    kept_half = jnp.where(upper == 1, by_bits[1], by_bits[0])
    sent_half = jnp.where(upper == 1, by_bits[0], by_bits[1])
    numerator, row_max, row_total = merge_level(kept_half, sent_half, 1)
    numerator, row_max, row_total = merge_level(numerator, numerator, 0)
    context_columns = (numerator / row_total[None]).astype(jnp.bfloat16)

    block_rows = query_total // (group_size)
    chips = nx * ny
    core_rows = chips * block_rows
    chip_columns = lax.dynamic_index_in_dim(
        context_columns.reshape(nc * column_width, chips, nc, block_rows), core, 2, keepdims=False
    ).reshape(nc * column_width, core_rows)
    outgoing = jnp.broadcast_to(chip_columns[None], (chips,) + chip_columns.shape)
    core_context = lax.all_to_all(outgoing, PLANE, 0, 0, tiled=True).reshape(
        group_size * column_width, core_rows
    )
    chip_width = nc * column_width
    column_bias = lax.dynamic_slice_in_dim(out_biases[0], chip * chip_width, chip_width)
    projected_part = (
        jnp.einsum("ct,cd->dt", core_context, chip_out, preferred_element_type=jnp.float32)
        + column_bias[:, None]
    ).astype(jnp.bfloat16)
    spread = jnp.broadcast_to(projected_part[None], (chips,) + projected_part.shape)
    spread, group_down = lax.optimization_barrier((spread, group_down))
    projected = lax.all_to_all(spread, PLANE, 0, 0, tiled=True).reshape(chips * chip_width, core_rows)
    core_tokens = lax.dynamic_index_in_dim(
        token_rows.reshape(chips, nc, block_rows, -1), core, axis=1, keepdims=False
    ).reshape(core_rows, -1)
    residual = core_tokens.T.astype(jnp.float32) + projected.astype(jnp.float32)
    centered = residual - jnp.mean(residual, axis=0, keepdims=True)
    variance = jnp.mean(centered * centered, axis=0, keepdims=True)
    normed_t = (
        centered * lax.rsqrt(variance + 1e-06) * norm_gains[0][:, None] + norm_biases[0][:, None]
    ).astype(jnp.bfloat16)
    inner = jax.nn.gelu(
        jnp.einsum("dt,df->tf", normed_t, chip_in, preferred_element_type=jnp.float32) + chip_in_bias,
        approximate=True,
    ).astype(jnp.bfloat16)
    group_inner = lax.all_to_all(
        jnp.broadcast_to(inner[None], (nx,) + inner.shape), "bx", 0, 0, tiled=True
    ).reshape(nx, core_rows, nc, hidden_width)
    mixed_parts = jnp.einsum(
        "xtcf,xcdf->td", group_inner, group_down, preferred_element_type=jnp.float32
    )
    from_chips = lax.all_to_all(
        mixed_parts.reshape(chips, block_rows, quarter_width), PLANE, 0, 0, tiled=True
    ).reshape(nx, ny, block_rows, quarter_width)
    mixed_rows = from_chips.sum(axis=1).transpose(1, 0, 2).reshape(block_rows, d_model)
    own_normed = lax.dynamic_slice_in_dim(normed_t, chip * block_rows, block_rows, 1).T
    layer_output = layer_norm(
        own_normed.astype(jnp.float32) + mixed_rows + out_biases[1], norm_gains[1], norm_biases[1]
    ).astype(jnp.bfloat16)
    return (layer_output[None], appended)


def solution(mesh):
    req, blk = mesh.devices.shape
    fine = Mesh(mesh.devices.reshape(req, 4, blk // 8, 2), ("req",) + BLK)
    return jax.shard_map(
        local,
        mesh=fine,
        in_specs=(
            P("req", None, None),
            P("req", BLK, None, None, None),
            P("req", None),
            P("req"),
            P("req", None),
            P("req", None, BLK),
            P(None, BLK),
            P("req", BLK),
            P("req", BLK),
            P(),
            P("req", BLK),
            P(),
            P(),
            P(),
        ),
        out_specs=(P("req", BLK, None), P("req", None, None, BLK)),
        check_vma=False,
    )
```

```python
import math

import jax
import jax.numpy as jnp
from jax import lax
from jax.sharding import Mesh
from jax.sharding import PartitionSpec as P

HEADS = 16
HEAD_DIM = 128


MASKED = -1e30
PLANE = ("bx", "by")
BLK = ("bx", "by", "bc")


def swap(axis, n):
    return [(i, i ^ 1) for i in range(n)]


def layer_norm(values, gain_row, shift_row):
    centered = values - jnp.mean(values, axis=-1, keepdims=True)
    variance = jnp.mean(centered * centered, axis=-1, keepdims=True)
    return centered * lax.rsqrt(variance + 1e-06) * gain_row + shift_row


def partial_block(queries, key_rows, value_rows, visible):
    scores = jnp.einsum("qd,kd->qk", queries, key_rows, preferred_element_type=jnp.float32) * (
        1.0 / math.sqrt(HEAD_DIM)
    )
    scores = jnp.where(visible, scores, MASKED)
    row_max = jnp.max(scores, axis=1)
    weights = jnp.where(visible, jnp.exp(scores - row_max[:, None]), 0.0)
    row_total = jnp.sum(weights, axis=1)
    numerator = jnp.einsum(
        "qk,kd->dq", weights.astype(jnp.bfloat16), value_rows, preferred_element_type=jnp.float32
    )
    return (numerator, row_max, row_total)


def merge_blocks(earlier_part, later_part):
    joined = jnp.maximum(earlier_part[1], later_part[1])
    scale_earlier = jnp.exp(earlier_part[1] - joined)
    scale_later = jnp.exp(later_part[1] - joined)
    numerator = earlier_part[0] * scale_earlier[:, None] + later_part[0] * scale_later[:, None]
    return (numerator, joined, earlier_part[2] * scale_earlier + later_part[2] * scale_later)


def gather_rows(block):
    reqs = lax.axis_size("req")
    spread = jnp.broadcast_to(block[None], (reqs,) + block.shape)
    return lax.all_to_all(spread, "req", 0, 0, tiled=True).reshape(reqs * block.shape[0], -1)


def core_pair(own, other, core, axis):
    return jnp.where(
        core == 0,
        jnp.concatenate([own, other], axis=axis),
        jnp.concatenate([other, own], axis=axis),
    )


def local(
    tokens,
    cache_entries,
    cache_tenants,
    cached_length,
    tenant_bounds,
    qkv_weight,
    qkv_bias,
    out_weight,
    in_weight,
    in_bias,
    down_weight,
    out_biases,
    norm_gains,
    norm_biases,
):
    nx, ny, nc = lax.axis_size("bx"), lax.axis_size("by"), lax.axis_size("bc")
    core = lax.axis_index("bc")
    chip = lax.axis_index("bx") * ny + lax.axis_index("by")
    block_index = chip * nc + core
    group_size = nx * ny * nc
    groups = group_size // HEADS
    low_bits = groups.bit_length() - 1
    group_index = block_index % groups

    rows, _, column_width = qkv_weight.shape
    qkv_flat = qkv_weight.reshape(rows, 3 * column_width)
    hidden_width = in_weight.shape[1]
    packed = jnp.concatenate([out_weight, in_weight, down_weight], axis=1)
    reqs = lax.axis_size("req")
    qkv_blocks = lax.all_to_all(
        jnp.broadcast_to(qkv_flat[None], (reqs,) + qkv_flat.shape), "req", 0, 0, tiled=True
    ).reshape(reqs, rows, 3, column_width)
    late = gather_rows(packed)
    front = late[:, : column_width + hidden_width]
    sibling = lax.ppermute(front, "bc", swap("bc", nc))
    chip_out = core_pair(front[:, :column_width], sibling[:, :column_width], core, 1)
    chip_in = core_pair(front[:, column_width:], sibling[:, column_width:], core, 1)
    chip_in_bias = lax.dynamic_slice_in_dim(in_bias, chip * nc * hidden_width, nc * hidden_width)
    d_model = late.shape[0]
    quarter_width = d_model // nx
    own_down = late[:, column_width + hidden_width :].reshape(nx, quarter_width, hidden_width)
    row = lax.axis_index("bx")
    received = [lax.dynamic_index_in_dim(own_down, row, 0, keepdims=False)]
    for k in range(1, nx):
        received.append(
            lax.ppermute(
                lax.dynamic_index_in_dim(own_down, row ^ k, 0, keepdims=False),
                "bx",
                [(i, i ^ k) for i in range(nx)],
            )
        )
    from_row = jnp.take(jnp.stack(received), row ^ jnp.arange(nx), axis=0)
    from_sibling = lax.ppermute(from_row, "bc", swap("bc", nc))
    group_down = core_pair(from_row[:, None], from_sibling[:, None], core, 1)

    query_total = tokens.shape[1]
    token_rows = tokens[0]
    qkv_columns = (
        jnp.einsum(
            "tsd,sdce->cet",
            token_rows.reshape(query_total, reqs, rows),
            qkv_blocks,
            preferred_element_type=jnp.float32,
        )
        + qkv_bias[:, :, None]
    ).astype(jnp.bfloat16)
    appended = qkv_columns[1:].transpose(2, 0, 1)[None]

    def from_partner(value, bit_level):
        if bit_level == 0:
            return lax.ppermute(value, "bc", swap("bc", nc))
        return lax.ppermute(value, "by", [(i, i ^ (1 << (bit_level - 1))) for i in range(ny)])

    upper = group_index >> 1 & 1
    partner = from_partner(qkv_columns, 1)
    head_qkv = jnp.where(
        upper == 1,
        jnp.stack([partner, qkv_columns], axis=1),
        jnp.stack([qkv_columns, partner], axis=1),
    )
    partner = from_partner(head_qkv, 0)
    head_qkv = jnp.where(
        core == 1, jnp.stack([partner, head_qkv], axis=2), jnp.stack([head_qkv, partner], axis=2)
    ).reshape(3, groups * column_width, query_total)
    queries = head_qkv[0].T
    fresh_count = query_total // groups
    fresh_start = group_index * fresh_count
    fresh_keys = lax.dynamic_slice_in_dim(head_qkv[1], fresh_start, fresh_count, 1).T
    fresh_values = lax.dynamic_slice_in_dim(head_qkv[2], fresh_start, fresh_count, 1).T
    cache_count = cache_entries.shape[2]
    cache_keys = cache_entries[0, 0, :, 0]
    cache_values = cache_entries[0, 0, :, 1]
    cache_position = group_index * cache_count + jnp.arange(cache_count, dtype=jnp.int32)
    tenant_slice = lax.dynamic_slice_in_dim(
        cache_tenants[0], group_index * cache_count, cache_count, 0
    )
    readable = (
        (cache_position < cached_length[0])
        & (tenant_slice >= tenant_bounds[0, 0])
        & (tenant_slice < tenant_bounds[0, 1])
    )
    query_position = jnp.arange(query_total, dtype=jnp.int32)
    fresh_position = fresh_start + jnp.arange(fresh_count, dtype=jnp.int32)
    fresh_visible = fresh_position[None, :] <= query_position[:, None]
    cache_visible = jnp.broadcast_to(readable[None, :], (query_total, cache_count))
    numerator, row_max, row_total = partial_block(
        queries,
        jnp.concatenate([cache_keys, fresh_keys], axis=0),
        jnp.concatenate([cache_values, fresh_values], axis=0),
        jnp.concatenate([cache_visible, fresh_visible], axis=1),
    )
    def merge_level(kept_half, sent_half, bit_level):
        sent = jnp.concatenate([sent_half, row_max[None], row_total[None]], axis=0)
        got_back = from_partner(sent, bit_level)
        other_sum, other_max, other_total = got_back[:-2], got_back[-2], got_back[-1]
        joined = jnp.maximum(row_max, other_max)
        scale_kept = jnp.exp(row_max - joined)
        scale_other = jnp.exp(other_max - joined)
        merged = kept_half * scale_kept[None] + other_sum * scale_other[None]
        return merged, joined, row_total * scale_kept + other_total * scale_other

    by_bits = numerator.reshape(2, 2 * column_width, query_total)
    kept_half = jnp.where(upper == 1, by_bits[1], by_bits[0])
    sent_half = jnp.where(upper == 1, by_bits[0], by_bits[1])
    numerator, row_max, row_total = merge_level(kept_half, sent_half, 1)
    numerator, row_max, row_total = merge_level(numerator, numerator, 0)
    context_columns = (numerator / row_total[None]).astype(jnp.bfloat16)

    block_rows = query_total // (group_size)
    chips = nx * ny
    core_rows = chips * block_rows
    chip_columns = lax.dynamic_index_in_dim(
        context_columns.reshape(nc * column_width, chips, nc, block_rows), core, 2, keepdims=False
    ).reshape(nc * column_width, core_rows)
    outgoing = jnp.broadcast_to(chip_columns[None], (chips,) + chip_columns.shape)
    core_context = lax.all_to_all(outgoing, PLANE, 0, 0, tiled=True).reshape(
        group_size * column_width, core_rows
    )
    chip_width = nc * column_width
    column_bias = lax.dynamic_slice_in_dim(out_biases[0], chip * chip_width, chip_width)
    projected_part = (
        jnp.einsum("ct,cd->dt", core_context, chip_out, preferred_element_type=jnp.float32)
        + column_bias[:, None]
    ).astype(jnp.bfloat16)
    spread = jnp.broadcast_to(projected_part[None], (chips,) + projected_part.shape)
    spread, group_down = lax.optimization_barrier((spread, group_down))
    projected = lax.all_to_all(spread, PLANE, 0, 0, tiled=True).reshape(chips * chip_width, core_rows)
    core_tokens = lax.dynamic_index_in_dim(
        token_rows.reshape(chips, nc, block_rows, -1), core, axis=1, keepdims=False
    ).reshape(core_rows, -1)
    normed = layer_norm(
        core_tokens.astype(jnp.float32) + projected.T.astype(jnp.float32),
        norm_gains[0],
        norm_biases[0],
    ).astype(jnp.bfloat16)
    inner = jax.nn.gelu(
        jnp.dot(normed, chip_in, preferred_element_type=jnp.float32) + chip_in_bias,
        approximate=True,
    ).astype(jnp.bfloat16)
    group_inner = lax.all_to_all(
        jnp.broadcast_to(inner[None], (nx,) + inner.shape), "bx", 0, 0, tiled=True
    ).reshape(nx, core_rows, nc, hidden_width)
    mixed_parts = jnp.einsum(
        "xtcf,xcdf->td", group_inner, group_down, preferred_element_type=jnp.float32
    )
    from_chips = lax.all_to_all(
        mixed_parts.reshape(chips, block_rows, quarter_width), PLANE, 0, 0, tiled=True
    ).reshape(nx, ny, block_rows, quarter_width)
    mixed_rows = from_chips.sum(axis=1).transpose(1, 0, 2).reshape(block_rows, d_model)
    own_normed = lax.dynamic_slice_in_dim(normed, chip * block_rows, block_rows, 0)
    layer_output = layer_norm(
        own_normed.astype(jnp.float32) + mixed_rows + out_biases[1], norm_gains[1], norm_biases[1]
    ).astype(jnp.bfloat16)
    return (layer_output[None], appended)


def solution(mesh):
    req, blk = mesh.devices.shape
    fine = Mesh(mesh.devices.reshape(req, 4, blk // 8, 2), ("req",) + BLK)
    return jax.shard_map(
        local,
        mesh=fine,
        in_specs=(
            P("req", None, None),
            P("req", BLK, None, None, None),
            P("req", None),
            P("req"),
            P("req", None),
            P("req", None, BLK),
            P(None, BLK),
            P("req", BLK),
            P("req", BLK),
            P(),
            P("req", BLK),
            P(),
            P(),
            P(),
        ),
        out_specs=(P("req", BLK, None), P("req", None, None, BLK)),
        check_vma=False,
    )
```

```python
import math

import jax
import jax.numpy as jnp
from jax import lax
from jax.sharding import Mesh
from jax.sharding import PartitionSpec as P

HEADS = 16
HEAD_DIM = 128


MASKED = -1e30
PLANE = ("bx", "by")
BLK = ("bx", "by", "bc")


def swap(axis, n):
    return [(i, i ^ 1) for i in range(n)]


def layer_norm(values, gain_row, shift_row):
    centered = values - jnp.mean(values, axis=-1, keepdims=True)
    variance = jnp.mean(centered * centered, axis=-1, keepdims=True)
    return centered * lax.rsqrt(variance + 1e-06) * gain_row + shift_row


def partial_block(queries, key_rows, value_rows, visible):
    scores = jnp.einsum("qd,kd->qk", queries, key_rows, preferred_element_type=jnp.float32) * (
        1.0 / math.sqrt(HEAD_DIM)
    )
    scores = jnp.where(visible, scores, MASKED)
    row_max = jnp.max(scores, axis=1)
    weights = jnp.where(visible, jnp.exp(scores - row_max[:, None]), 0.0)
    row_total = jnp.sum(weights, axis=1)
    numerator = jnp.einsum(
        "qk,kd->dq", weights.astype(jnp.bfloat16), value_rows, preferred_element_type=jnp.float32
    )
    return (numerator, row_max, row_total)


def merge_blocks(earlier_part, later_part):
    joined = jnp.maximum(earlier_part[1], later_part[1])
    scale_earlier = jnp.exp(earlier_part[1] - joined)
    scale_later = jnp.exp(later_part[1] - joined)
    numerator = earlier_part[0] * scale_earlier[:, None] + later_part[0] * scale_later[:, None]
    return (numerator, joined, earlier_part[2] * scale_earlier + later_part[2] * scale_later)


def gather_rows(block):
    reqs = lax.axis_size("req")
    spread = jnp.broadcast_to(block[None], (reqs,) + block.shape)
    return lax.all_to_all(spread, "req", 0, 0, tiled=True).reshape(reqs * block.shape[0], -1)


def core_pair(own, other, core, axis):
    return jnp.where(
        core == 0,
        jnp.concatenate([own, other], axis=axis),
        jnp.concatenate([other, own], axis=axis),
    )


def local(
    tokens,
    cache_entries,
    cache_tenants,
    cached_length,
    tenant_bounds,
    qkv_weight,
    qkv_bias,
    out_weight,
    in_weight,
    in_bias,
    down_weight,
    out_biases,
    norm_gains,
    norm_biases,
):
    nx, ny, nc = lax.axis_size("bx"), lax.axis_size("by"), lax.axis_size("bc")
    core = lax.axis_index("bc")
    chip = lax.axis_index("bx") * ny + lax.axis_index("by")
    block_index = chip * nc + core
    group_size = nx * ny * nc
    groups = group_size // HEADS
    low_bits = groups.bit_length() - 1
    group_index = block_index % groups

    rows, _, column_width = qkv_weight.shape
    qkv_flat = qkv_weight.reshape(rows, 3 * column_width)
    hidden_width = in_weight.shape[1]
    packed = jnp.concatenate([out_weight, in_weight, down_weight], axis=1)
    reqs = lax.axis_size("req")
    qkv_blocks = lax.all_to_all(
        jnp.broadcast_to(qkv_flat[None], (reqs,) + qkv_flat.shape), "req", 0, 0, tiled=True
    ).reshape(reqs, rows, 3, column_width)
    late = gather_rows(packed)
    front = late[:, : column_width + hidden_width]
    sibling = lax.ppermute(front, "bc", swap("bc", nc))
    chip_out = core_pair(front[:, :column_width], sibling[:, :column_width], core, 1)
    chip_in = core_pair(front[:, column_width:], sibling[:, column_width:], core, 1)
    chip_in_bias = lax.dynamic_slice_in_dim(in_bias, chip * nc * hidden_width, nc * hidden_width)
    d_model = late.shape[0]
    quarter_width = d_model // nx
    own_down = late[:, column_width + hidden_width :].reshape(nx, quarter_width, hidden_width)
    row = lax.axis_index("bx")
    received = [lax.dynamic_index_in_dim(own_down, row, 0, keepdims=False)]
    for k in range(1, nx):
        received.append(
            lax.ppermute(
                lax.dynamic_index_in_dim(own_down, row ^ k, 0, keepdims=False),
                "bx",
                [(i, i ^ k) for i in range(nx)],
            )
        )
    from_row = jnp.take(jnp.stack(received), row ^ jnp.arange(nx), axis=0)
    from_sibling = lax.ppermute(from_row, "bc", swap("bc", nc))
    group_down = core_pair(from_row[:, None], from_sibling[:, None], core, 1)

    query_total = tokens.shape[1]
    token_rows = tokens[0]
    qkv_columns = (
        jnp.einsum(
            "tsd,sdce->cet",
            token_rows.reshape(query_total, reqs, rows),
            qkv_blocks,
            preferred_element_type=jnp.float32,
        )
        + qkv_bias[:, :, None]
    ).astype(jnp.bfloat16)
    appended = qkv_columns[1:].transpose(2, 0, 1)[None]

    def from_partner(value, bit_level):
        if bit_level == 0:
            return lax.ppermute(value, "bc", swap("bc", nc))
        return lax.ppermute(value, "by", [(i, i ^ (1 << (bit_level - 1))) for i in range(ny)])

    upper = group_index >> 1 & 1
    partner = from_partner(qkv_columns, 1)
    head_qkv = jnp.where(
        upper == 1,
        jnp.stack([partner, qkv_columns], axis=1),
        jnp.stack([qkv_columns, partner], axis=1),
    )
    partner = from_partner(head_qkv, 0)
    head_qkv = jnp.where(
        core == 1, jnp.stack([partner, head_qkv], axis=2), jnp.stack([head_qkv, partner], axis=2)
    ).reshape(3, groups * column_width, query_total)
    queries = head_qkv[0].T
    fresh_count = query_total // groups
    fresh_start = group_index * fresh_count
    fresh_keys = lax.dynamic_slice_in_dim(head_qkv[1], fresh_start, fresh_count, 1).T
    fresh_values = lax.dynamic_slice_in_dim(head_qkv[2], fresh_start, fresh_count, 1).T
    cache_count = cache_entries.shape[2]
    cache_keys = cache_entries[0, 0, :, 0]
    cache_values = cache_entries[0, 0, :, 1]
    cache_position = group_index * cache_count + jnp.arange(cache_count, dtype=jnp.int32)
    tenant_slice = lax.dynamic_slice_in_dim(
        cache_tenants[0], group_index * cache_count, cache_count, 0
    )
    readable = (
        (cache_position < cached_length[0])
        & (tenant_slice >= tenant_bounds[0, 0])
        & (tenant_slice < tenant_bounds[0, 1])
    )
    query_position = jnp.arange(query_total, dtype=jnp.int32)
    fresh_position = fresh_start + jnp.arange(fresh_count, dtype=jnp.int32)
    fresh_visible = fresh_position[None, :] <= query_position[:, None]
    cache_visible = jnp.broadcast_to(readable[None, :], (query_total, cache_count))
    numerator, row_max, row_total = partial_block(
        queries,
        jnp.concatenate([cache_keys, fresh_keys], axis=0),
        jnp.concatenate([cache_values, fresh_values], axis=0),
        jnp.concatenate([cache_visible, fresh_visible], axis=1),
    )
    def merge_level(kept_half, sent_half, bit_level):
        sent = jnp.concatenate([sent_half, row_max[None], row_total[None]], axis=0)
        got_back = from_partner(sent, bit_level)
        other_sum, other_max, other_total = got_back[:-2], got_back[-2], got_back[-1]
        joined = jnp.maximum(row_max, other_max)
        scale_kept = jnp.exp(row_max - joined)
        scale_other = jnp.exp(other_max - joined)
        merged = kept_half * scale_kept[None] + other_sum * scale_other[None]
        return merged, joined, row_total * scale_kept + other_total * scale_other

    by_bits = numerator.reshape(2, 2 * column_width, query_total)
    kept_half = jnp.where(upper == 1, by_bits[1], by_bits[0])
    sent_half = jnp.where(upper == 1, by_bits[0], by_bits[1])
    numerator, row_max, row_total = merge_level(kept_half, sent_half, 1)
    numerator, row_max, row_total = merge_level(numerator, numerator, 0)
    context_columns = (numerator / row_total[None]).astype(jnp.bfloat16)

    block_rows = query_total // (group_size)
    chips = nx * ny
    core_rows = chips * block_rows
    chip_columns = lax.dynamic_index_in_dim(
        context_columns.reshape(nc * column_width, chips, nc, block_rows), core, 2, keepdims=False
    ).reshape(nc * column_width, core_rows)
    outgoing = jnp.broadcast_to(chip_columns[None], (chips,) + chip_columns.shape)
    core_context = lax.all_to_all(outgoing, PLANE, 0, 0, tiled=True).reshape(
        group_size * column_width, core_rows
    )
    chip_width = nc * column_width
    column_bias = lax.dynamic_slice_in_dim(out_biases[0], chip * chip_width, chip_width)
    projected_part = (
        jnp.einsum("ct,cd->dt", core_context, chip_out, preferred_element_type=jnp.float32)
        + column_bias[:, None]
    ).astype(jnp.bfloat16)
    spread = jnp.broadcast_to(projected_part[None], (chips,) + projected_part.shape)
    spread, group_down = lax.optimization_barrier((spread, group_down))
    projected = lax.all_to_all(spread, PLANE, 0, 0, tiled=True).reshape(chips * chip_width, core_rows)
    core_tokens = lax.dynamic_index_in_dim(
        token_rows.reshape(chips, nc, block_rows, -1), core, axis=1, keepdims=False
    ).reshape(core_rows, -1)
    normed = layer_norm(
        core_tokens.astype(jnp.float32) + lax.optimization_barrier(projected.T).astype(jnp.float32),
        norm_gains[0],
        norm_biases[0],
    ).astype(jnp.bfloat16)
    inner = jax.nn.gelu(
        jnp.dot(normed, chip_in, preferred_element_type=jnp.float32) + chip_in_bias,
        approximate=True,
    ).astype(jnp.bfloat16)
    group_inner = lax.all_to_all(
        jnp.broadcast_to(inner[None], (nx,) + inner.shape), "bx", 0, 0, tiled=True
    ).reshape(nx, core_rows, nc, hidden_width)
    mixed_parts = jnp.einsum(
        "xtcf,xcdf->td", group_inner, group_down, preferred_element_type=jnp.float32
    )
    from_chips = lax.all_to_all(
        mixed_parts.reshape(chips, block_rows, quarter_width), PLANE, 0, 0, tiled=True
    ).reshape(nx, ny, block_rows, quarter_width)
    mixed_rows = from_chips.sum(axis=1).transpose(1, 0, 2).reshape(block_rows, d_model)
    own_normed = lax.dynamic_slice_in_dim(normed, chip * block_rows, block_rows, 0)
    layer_output = layer_norm(
        own_normed.astype(jnp.float32) + mixed_rows + out_biases[1], norm_gains[1], norm_biases[1]
    ).astype(jnp.bfloat16)
    return (layer_output[None], appended)


def solution(mesh):
    req, blk = mesh.devices.shape
    fine = Mesh(mesh.devices.reshape(req, 4, blk // 8, 2), ("req",) + BLK)
    return jax.shard_map(
        local,
        mesh=fine,
        in_specs=(
            P("req", None, None),
            P("req", BLK, None, None, None),
            P("req", None),
            P("req"),
            P("req", None),
            P("req", None, BLK),
            P(None, BLK),
            P("req", BLK),
            P("req", BLK),
            P(),
            P("req", BLK),
            P(),
            P(),
            P(),
        ),
        out_specs=(P("req", BLK, None), P("req", None, None, BLK)),
        check_vma=False,
    )
```
